256 devices in a mesh: gx: 16 (over z, core), gy: 16 (over y, x).
Axes of the slice: x: 4, y: 4, z: 8, core: 2. Of those that a mesh axis runs over, the one named last changes fastest.
Arguments:
- field: float32 [64, 4096, 128], P('gy', 'gx'), may hold values from -5 to 5
- courant: float32 [3, 64, 4096, 128], P(None, 'gy', 'gx'), may hold values from -2.5 to 2.5
- diffusion_number: float32 [64, 4096, 128], P('gy', 'gx'), may hold values from 65536 to 1310720
Outputs:
- solved: float32 [64, 4096, 128], P('gy', 'gx')
The draws below stay inside these ranges and needn't reach their ends.
All inputs are finite; a program needn't handle non-finite values.
Results may differ from the reference program's by a relative error of at most 0.0013.
Values sent between devices are 32-bit elements; how exact they have to be, the bound alone decides.
No kernel may reach another device: no remote copies, remote signals or barrier semaphores. Data moves between devices by JAX's collectives and lax.ppermute only.
A program may use at most 64 MiB of HBM per device.

```python
import math
import jax
import jax.numpy as jnp
from jax import lax

NZ = 128
NX = 4096
NY = 64


def level_of(own_key, extent, cuts, least, high):
    level, own = 1.0, jax.random.fold_in(own_key, 6)
    for axis_at, parts in cuts:
        heights = jnp.exp(jax.random.uniform(jax.random.fold_in(own, axis_at), (parts,), jnp.float32, least / len(cuts), high / len(cuts)))
        level = level * jnp.repeat(heights, extent[axis_at] // parts).reshape([-1 if axis == axis_at else 1 for axis in range(len(extent))])
    return level


def noise(rng, shape, width, most, pieces=(), held_as=jnp.bfloat16):
    values = jax.random.normal(rng, shape, jnp.float32) * width
    if len(pieces) > 0:
        values = level_of(rng, shape, pieces, -0.22, 0.18) * values
    return jnp.clip(values, min=-most, max=most).astype(held_as)


def setup_inputs(seed: int = 0) -> dict:
    arg_keys = jax.random.split(jax.random.key(seed), 4)
    field = noise(arg_keys[0], (NY, NX, NZ), 1.0, 5.0, ((0, 16), (1, 16)), jnp.float32)
    courant = noise(arg_keys[1], (3, NY, NX, NZ), 0.5, 2.5, ((1, 16), (2, 16)), jnp.float32)
    diffusion_number = jnp.clip(jnp.exp(math.log(1310720) - 2.9957323 * jax.random.uniform(arg_keys[2], (NY, NX, NZ), jnp.float32) ** level_of(arg_keys[2], (NY, NX, NZ), ((0, 16), (1, 16)), -0.2, 0.2)), 65536.0, 1310720)
    return dict(field=field, courant=courant, diffusion_number=diffusion_number)


def difference_pair(padded, sweep_direction, length):
    shifted = [lax.slice_in_dim(padded, offset, offset + length, axis=sweep_direction) for offset in range(5)]
    gradient = (8.0 * (shifted[3] - shifted[1]) - (shifted[4] - shifted[0])) / 12.0
    curvature = (16.0 * (shifted[3] + shifted[1]) - (shifted[4] + shifted[0]) - 30.0 * shifted[2]) / 12.0
    return gradient, curvature


def build_rhs(field, courant, y_padded, x_padded):
    z_padded = jnp.concatenate([field[:, :, -2:], field, field[:, :, :2]], 2)
    grad_y, curve_y = difference_pair(y_padded, 0, field.shape[0])
    grad_x = difference_pair(x_padded, 1, field.shape[1])[0]
    grad_z, curve_z = difference_pair(z_padded, 2, field.shape[2])
    transport = courant[0] * grad_x + courant[1] * grad_y + courant[2] * grad_z
    return field - transport + 0.05 * (curve_y + curve_z) + 0.3 * field / (1.0 + field * field)


def reference(field, courant, diffusion_number):
    y_padded = jnp.concatenate([field[-2:], field, field[:2]], 0)
    x_padded = jnp.pad(field, ((0, 0), (2, 2), (0, 0)))
    rhs = build_rhs(field, courant, y_padded, x_padded)
    rates = jnp.moveaxis(diffusion_number, 1, 0)
    right_hand_sides = jnp.moveaxis(rhs, 1, 0)
    lower_band = -rates
    main_diagonal = 1.0 + 2.0 * rates
    upper_band = -rates

    def forward(carry, row_set):
        prev_ratio, prev_value = carry
        low_coef, mid_coef, high_coef, value = row_set
        denom = mid_coef - low_coef * prev_ratio
        ratio = high_coef / denom
        reduced = (value - low_coef * prev_value) / denom
        return (ratio, reduced), (ratio, reduced)

    start = (jnp.zeros_like(right_hand_sides[0]), jnp.zeros_like(right_hand_sides[0]))
    unused, (ratios, values) = lax.scan(forward, start, (lower_band, main_diagonal, upper_band, right_hand_sides))

    def backward(following, row_set):
        ratio, value = row_set
        result = value - ratio * following
        return result, result

    unused_last, solution = lax.scan(backward, jnp.zeros_like(right_hand_sides[0]), (ratios, values), reverse=True)
    return jnp.moveaxis(solution, 0, 1)
```

```python
import jax
import jax.numpy as jnp
from jax import lax
from jax.sharding import PartitionSpec as P


def padded_2(cells, sides, width, closed):
    for axis, dim in sides:
        count = lax.axis_size(axis)
        ends = count if closed else count - 1
        head = lax.slice_in_dim(cells, 0, width, axis=dim)
        tail = lax.slice_in_dim(cells, cells.shape[dim] - width, cells.shape[dim], axis=dim)
        cells = jnp.concatenate(
            [
                lax.ppermute(tail, axis, [(i, (i + 1) % count) for i in range(ends)]),
                cells,
                lax.ppermute(head, axis, [((i + 1) % count, i) for i in range(ends)]),
            ],
            axis=dim,
        )
    return cells


def difference_pair(padded, sweep_direction, length):
    shifted = [
        lax.slice_in_dim(padded, offset, offset + length, axis=sweep_direction)
        for offset in range(5)
    ]
    gradient = (8.0 * (shifted[3] - shifted[1]) - (shifted[4] - shifted[0])) / 12.0
    curvature = (
        16.0 * (shifted[3] + shifted[1]) - (shifted[4] + shifted[0]) - 30.0 * shifted[2]
    ) / 12.0
    return (gradient, curvature)


def build_rhs(field, courant, y_padded, x_padded):
    z_padded = jnp.concatenate([field[:, :, -2:], field, field[:, :, :2]], 2)
    grad_y, curve_y = difference_pair(y_padded, 0, field.shape[0])
    grad_x = difference_pair(x_padded, 1, field.shape[1])[0]
    grad_z, curve_z = difference_pair(z_padded, 2, field.shape[2])
    transport = courant[0] * grad_x + courant[1] * grad_y + courant[2] * grad_z
    return field - transport + 0.05 * (curve_y + curve_z) + 0.3 * field / (1.0 + field * field)


def rows_below(values, stride, fill, sweep_direction):
    length = values.shape[sweep_direction]
    filler = jnp.full_like(lax.slice_in_dim(values, 0, stride, axis=sweep_direction), fill)
    return jnp.concatenate(
        [filler, lax.slice_in_dim(values, 0, length - stride, axis=sweep_direction)],
        sweep_direction,
    )


def rows_above(values, stride, fill, sweep_direction):
    length = values.shape[sweep_direction]
    filler = jnp.full_like(
        lax.slice_in_dim(values, length - stride, length, axis=sweep_direction), fill
    )
    return jnp.concatenate(
        [lax.slice_in_dim(values, stride, length, axis=sweep_direction), filler], sweep_direction
    )


def combine_rows(own_rows, below_set, above_set):
    lower_band, main_diagonal, upper_band, right_hand_sides = own_rows
    low_sub, low_diag, low_super, low_rights = below_set
    high_sub, high_diag, high_super, high_rights = above_set
    factor_low = -lower_band / low_diag
    factor_high = -upper_band / high_diag
    new_sub = factor_low * low_sub
    new_super = factor_high * high_super
    new_diag = main_diagonal + factor_low * low_super + factor_high * high_sub
    new_rights = tuple(
        (
            value + factor_low * lower_value + factor_high * upper_value
            for value, lower_value, upper_value in zip(right_hand_sides, low_rights, high_rights)
        )
    )
    return (new_sub, new_diag, new_super, new_rights)


def parallel_cyclic_reduction(
    lower_band, main_diagonal, upper_band, right_hand_sides, sweep_direction
):
    length = main_diagonal.shape[sweep_direction]
    stride = 1
    while stride < length:
        below_set = (
            rows_below(lower_band, stride, 0.0, sweep_direction),
            rows_below(main_diagonal, stride, 1.0, sweep_direction),
            rows_below(upper_band, stride, 0.0, sweep_direction),
            tuple((rows_below(value, stride, 0.0, sweep_direction) for value in right_hand_sides)),
        )
        above_set = (
            rows_above(lower_band, stride, 0.0, sweep_direction),
            rows_above(main_diagonal, stride, 1.0, sweep_direction),
            rows_above(upper_band, stride, 0.0, sweep_direction),
            tuple((rows_above(value, stride, 0.0, sweep_direction) for value in right_hand_sides)),
        )
        lower_band, main_diagonal, upper_band, right_hand_sides = combine_rows(
            (lower_band, main_diagonal, upper_band, right_hand_sides), below_set, above_set
        )
        stride = stride * 2
    return tuple((value / main_diagonal for value in right_hand_sides))


def shards(field, courant, diffusion_number):
    y_padded = padded_2(field, (("gy", 0),), 2, True)
    x_padded = padded_2(field, (("gx", 1),), 2, False)
    rhs = build_rhs(field, courant, y_padded, x_padded)
    place = lax.axis_index("gx")
    device_count = lax.axis_size("gx")
    sub_full = -diffusion_number
    diag_full = 1.0 + 2.0 * diffusion_number
    super_full = -diffusion_number
    edge_zeros = jnp.zeros_like(rhs[:, 0:1])
    inner_zeros = jnp.zeros_like(rhs[:, 3:])
    sub_inner = jnp.concatenate([edge_zeros, sub_full[:, 2:-1]], 1)
    super_inner = jnp.concatenate([super_full[:, 1:-2], edge_zeros], 1)
    diag_inner = diag_full[:, 1:-1]
    first_unit = jnp.concatenate([-sub_full[:, 1:2], inner_zeros], 1)
    last_unit = jnp.concatenate([inner_zeros, -super_full[:, -2:-1]], 1)
    particular_solution, first_row_response, last_row_response = parallel_cyclic_reduction(
        sub_inner, diag_inner, super_inner, (rhs[:, 1:-1], first_unit, last_unit), 1
    )
    low_open = (place > 0).astype(jnp.float32)
    high_open = (place < device_count - 1).astype(jnp.float32)
    sub_first = sub_full[:, 0:1] * low_open
    diag_first = diag_full[:, 0:1] + super_full[:, 0:1] * first_row_response[:, 0:1]
    super_first = super_full[:, 0:1] * last_row_response[:, 0:1]
    right_first = rhs[:, 0:1] - super_full[:, 0:1] * particular_solution[:, 0:1]
    sub_last = sub_full[:, -1:] * first_row_response[:, -1:]
    diag_last = diag_full[:, -1:] + sub_full[:, -1:] * last_row_response[:, -1:]
    super_last = super_full[:, -1:] * high_open
    right_last = rhs[:, -1:] - sub_full[:, -1:] * particular_solution[:, -1:]
    reduced_sub = jnp.concatenate([sub_first, sub_last], 1)
    reduced_diag = jnp.concatenate([diag_first, diag_last], 1)
    reduced_super = jnp.concatenate([super_first, super_last], 1)
    reduced_right = jnp.concatenate([right_first, right_last], 1)
    stacked = jnp.concatenate([reduced_sub, reduced_diag, reduced_super, reduced_right], 1)
    gathered = lax.all_gather(stacked, "gx", axis=1, tiled=True)
    gathered = gathered.reshape(gathered.shape[0], device_count, 4, 2, gathered.shape[-1])
    gathered_lower_band, gathered_diagonal, gathered_upper_band, gathered_rhs = (
        gathered[:, :, k].reshape(gathered.shape[0], 2 * device_count, gathered.shape[-1])
        for k in range(4)
    )
    boundary_rows_gathered = parallel_cyclic_reduction(
        gathered_lower_band, gathered_diagonal, gathered_upper_band, (gathered_rhs,), 1
    )[0]
    ends = lax.dynamic_slice_in_dim(boundary_rows_gathered, 2 * place, 2, 1)
    interior = (
        particular_solution + first_row_response * ends[:, 0:1] + last_row_response * ends[:, 1:2]
    )
    return jnp.concatenate([ends[:, 0:1], interior, ends[:, 1:2]], 1)


def solution(mesh):
    in_specs = (P("gy", "gx", None), P(None, "gy", "gx", None), P("gy", "gx", None))
    out_specs = P("gy", "gx", None)
    return jax.shard_map(shards, mesh=mesh, in_specs=in_specs, out_specs=out_specs, check_vma=False)
```

```python
import jax
import jax.numpy as jnp
from jax import lax
from jax.sharding import PartitionSpec as P
from jax.experimental import pallas as pl
from jax.experimental.pallas import tpu as pltpu


def padded_2(cells, sides, width, closed):
    for axis, dim in sides:
        count = lax.axis_size(axis)
        ends = count if closed else count - 1
        head = lax.slice_in_dim(cells, 0, width, axis=dim)
        tail = lax.slice_in_dim(cells, cells.shape[dim] - width, cells.shape[dim], axis=dim)
        cells = jnp.concatenate(
            [
                lax.ppermute(tail, axis, [(i, (i + 1) % count) for i in range(ends)]),
                cells,
                lax.ppermute(head, axis, [((i + 1) % count, i) for i in range(ends)]),
            ],
            axis=dim,
        )
    return cells


def difference_pair(padded, sweep_direction, length):
    shifted = [
        lax.slice_in_dim(padded, offset, offset + length, axis=sweep_direction)
        for offset in range(5)
    ]
    gradient = (8.0 * (shifted[3] - shifted[1]) - (shifted[4] - shifted[0])) / 12.0
    curvature = (
        16.0 * (shifted[3] + shifted[1]) - (shifted[4] + shifted[0]) - 30.0 * shifted[2]
    ) / 12.0
    return (gradient, curvature)


def build_rhs(field, courant, y_padded, x_padded):
    z_padded = jnp.concatenate([field[:, :, -2:], field, field[:, :, :2]], 2)
    grad_y, curve_y = difference_pair(y_padded, 0, field.shape[0])
    grad_x = difference_pair(x_padded, 1, field.shape[1])[0]
    grad_z, curve_z = difference_pair(z_padded, 2, field.shape[2])
    transport = courant[0] * grad_x + courant[1] * grad_y + courant[2] * grad_z
    return field - transport + 0.05 * (curve_y + curve_z) + 0.3 * field / (1.0 + field * field)


def rows_below(values, stride, fill, sweep_direction):
    length = values.shape[sweep_direction]
    filler = jnp.full_like(lax.slice_in_dim(values, 0, stride, axis=sweep_direction), fill)
    return jnp.concatenate(
        [filler, lax.slice_in_dim(values, 0, length - stride, axis=sweep_direction)],
        sweep_direction,
    )


def rows_above(values, stride, fill, sweep_direction):
    length = values.shape[sweep_direction]
    filler = jnp.full_like(
        lax.slice_in_dim(values, length - stride, length, axis=sweep_direction), fill
    )
    return jnp.concatenate(
        [lax.slice_in_dim(values, stride, length, axis=sweep_direction), filler], sweep_direction
    )


def combine_rows(own_rows, below_set, above_set):
    lower_band, main_diagonal, upper_band, right_hand_sides = own_rows
    low_sub, low_diag, low_super, low_rights = below_set
    high_sub, high_diag, high_super, high_rights = above_set
    factor_low = -lower_band / low_diag
    factor_high = -upper_band / high_diag
    new_sub = factor_low * low_sub
    new_super = factor_high * high_super
    new_diag = main_diagonal + factor_low * low_super + factor_high * high_sub
    new_rights = tuple(
        (
            value + factor_low * lower_value + factor_high * upper_value
            for value, lower_value, upper_value in zip(right_hand_sides, low_rights, high_rights)
        )
    )
    return (new_sub, new_diag, new_super, new_rights)


def parallel_cyclic_reduction(
    lower_band, main_diagonal, upper_band, right_hand_sides, sweep_direction
):
    length = main_diagonal.shape[sweep_direction]
    stride = 1
    while stride < length:
        below_set = (
            rows_below(lower_band, stride, 0.0, sweep_direction),
            rows_below(main_diagonal, stride, 1.0, sweep_direction),
            rows_below(upper_band, stride, 0.0, sweep_direction),
            tuple((rows_below(value, stride, 0.0, sweep_direction) for value in right_hand_sides)),
        )
        above_set = (
            rows_above(lower_band, stride, 0.0, sweep_direction),
            rows_above(main_diagonal, stride, 1.0, sweep_direction),
            rows_above(upper_band, stride, 0.0, sweep_direction),
            tuple((rows_above(value, stride, 0.0, sweep_direction) for value in right_hand_sides)),
        )
        lower_band, main_diagonal, upper_band, right_hand_sides = combine_rows(
            (lower_band, main_diagonal, upper_band, right_hand_sides), below_set, above_set
        )
        stride = stride * 2
    return tuple((value / main_diagonal for value in right_hand_sides))


def to_chunks(values, chunks):
    planes, length, lanes = values.shape
    values = values.reshape(planes, chunks, length // chunks, lanes)
    return values.transpose(2, 1, 0, 3).reshape(length // chunks, chunks * planes, lanes)


def from_chunks(values, chunks):
    rows, sublanes, lanes = values.shape
    planes = sublanes // chunks
    values = values.reshape(rows, chunks, planes, lanes).transpose(2, 1, 0, 3)
    return values.reshape(planes, chunks * rows, lanes)


def thomas_kernel(rate_ref, right_ref, part_ref, first_ref, last_ref, ratio_ref):
    rows = rate_ref.shape[0]
    zero = jnp.zeros(rate_ref.shape[1:], jnp.float32)
    rate = rate_ref[1]
    inverse = 1.0 / (1.0 + 2.0 * rate)
    ratio = -rate * inverse
    part = right_ref[1] * inverse
    first = rate * inverse
    ratio_ref[1] = ratio
    part_ref[1] = part
    first_ref[1] = first

    def forward(i, carry):
        ratio, part, first, _ = carry
        rate = rate_ref[i]
        inverse = 1.0 / ((1.0 + 2.0 * rate) + rate * ratio)
        ratio = -rate * inverse
        part = (right_ref[i] + rate * part) * inverse
        first = rate * first * inverse
        ratio_ref[i] = ratio
        part_ref[i] = part
        first_ref[i] = first
        return ratio, part, first, inverse

    _, part, first, inverse = lax.fori_loop(
        2, rows - 1, forward, (ratio, part, first, zero), unroll=8
    )
    last = rate_ref[rows - 2] * inverse
    last_ref[rows - 2] = last

    def backward(j, carry):
        part, first, last = carry
        i = rows - 3 - j
        ratio = ratio_ref[i]
        part = part_ref[i] - ratio * part
        first = first_ref[i] - ratio * first
        last = -ratio * last
        part_ref[i] = part
        first_ref[i] = first
        last_ref[i] = last
        return part, first, last

    lax.fori_loop(0, rows - 3, backward, (part, first, last), unroll=8)
    for ref in (part_ref, first_ref, last_ref):
        ref[0] = zero
        ref[rows - 1] = zero


def local_solve(rate, right):
    shape = jax.ShapeDtypeStruct(rate.shape, jnp.float32)
    return pl.pallas_call(
        thomas_kernel,
        out_shape=(shape, shape, shape),
        scratch_shapes=[pltpu.VMEM(rate.shape, jnp.float32)],
    )(rate, right)


def shards(field, courant, diffusion_number):
    chunks = 2
    y_padded = padded_2(field, (("gy", 0),), 2, True)
    x_padded = padded_2(field, (("gx", 1),), 2, False)
    rhs = build_rhs(field, courant, y_padded, x_padded)
    place = lax.axis_index("gx")
    device_count = lax.axis_size("gx")
    planes = field.shape[0]
    rate = to_chunks(diffusion_number, chunks)
    right = to_chunks(rhs, chunks)
    part, first, last = local_solve(rate, right)
    rows = rate.shape[0]
    low_open = (place > 0).astype(jnp.float32)
    high_open = (place < device_count - 1).astype(jnp.float32)
    chunk_of = lax.broadcasted_iota(jnp.int32, (chunks, planes, 1), 0).reshape(chunks * planes, 1)
    low_scale = jnp.where(chunk_of == 0, low_open, 1.0)
    high_scale = jnp.where(chunk_of == chunks - 1, high_open, 1.0)
    rate_first, rate_last = rate[0], rate[rows - 1]
    sub_first = -rate_first * low_scale
    diag_first = (1.0 + 2.0 * rate_first) - rate_first * first[1]
    super_first = -rate_first * last[1]
    right_first = right[0] + rate_first * part[1]
    sub_last = -rate_last * first[rows - 2]
    diag_last = (1.0 + 2.0 * rate_last) - rate_last * last[rows - 2]
    super_last = -rate_last * high_scale
    right_last = right[rows - 1] + rate_last * part[rows - 2]
    stacked = jnp.stack(
        [sub_first, sub_last, diag_first, diag_last, super_first, super_last, right_first, right_last]
    )
    lanes = stacked.shape[-1]
    stacked = stacked.reshape(8, chunks, planes, lanes).transpose(2, 1, 0, 3)
    stacked = stacked.reshape(planes, chunks * 8, lanes)
    gathered = lax.all_gather(stacked, "gx", axis=1, tiled=True)
    gathered = gathered.reshape(planes, device_count, chunks, 4, 2, lanes)
    gathered_lower_band, gathered_diagonal, gathered_upper_band, gathered_rhs = (
        gathered[:, :, :, k].reshape(planes, 2 * chunks * device_count, lanes) for k in range(4)
    )
    boundary_rows_gathered = parallel_cyclic_reduction(
        gathered_lower_band, gathered_diagonal, gathered_upper_band, (gathered_rhs,), 1
    )[0]
    ends = lax.dynamic_slice_in_dim(boundary_rows_gathered, 2 * chunks * place, 2 * chunks, 1)
    ends = ends.reshape(planes, chunks, 2, lanes).transpose(2, 1, 0, 3)
    ends = ends.reshape(2, chunks * planes, lanes)
    start_value, end_value = ends[0], ends[1]
    solved = part + first * start_value[None] + last * end_value[None]
    row = lax.broadcasted_iota(jnp.int32, (rows, 1, 1), 0)
    solved = jnp.where(row == 0, start_value[None], solved)
    solved = jnp.where(row == rows - 1, end_value[None], solved)
    return from_chunks(solved, chunks)


def solution(mesh):
    in_specs = (P("gy", "gx", None), P(None, "gy", "gx", None), P("gy", "gx", None))
    out_specs = P("gy", "gx", None)
    return jax.shard_map(shards, mesh=mesh, in_specs=in_specs, out_specs=out_specs, check_vma=False)
```

```python
import jax
import jax.numpy as jnp
from jax import lax
from jax.sharding import PartitionSpec as P
from jax.experimental import pallas as pl
from jax.experimental.pallas import tpu as pltpu


def padded_2(cells, sides, width, closed):
    for axis, dim in sides:
        count = lax.axis_size(axis)
        ends = count if closed else count - 1
        head = lax.slice_in_dim(cells, 0, width, axis=dim)
        tail = lax.slice_in_dim(cells, cells.shape[dim] - width, cells.shape[dim], axis=dim)
        cells = jnp.concatenate(
            [
                lax.ppermute(tail, axis, [(i, (i + 1) % count) for i in range(ends)]),
                cells,
                lax.ppermute(head, axis, [((i + 1) % count, i) for i in range(ends)]),
            ],
            axis=dim,
        )
    return cells


def difference_pair(padded, sweep_direction, length):
    shifted = [
        lax.slice_in_dim(padded, offset, offset + length, axis=sweep_direction)
        for offset in range(5)
    ]
    gradient = (8.0 * (shifted[3] - shifted[1]) - (shifted[4] - shifted[0])) / 12.0
    curvature = (
        16.0 * (shifted[3] + shifted[1]) - (shifted[4] + shifted[0]) - 30.0 * shifted[2]
    ) / 12.0
    return (gradient, curvature)


def build_rhs(field, courant, y_padded, x_padded):
    z_padded = jnp.concatenate([field[:, :, -2:], field, field[:, :, :2]], 2)
    grad_y, curve_y = difference_pair(y_padded, 0, field.shape[0])
    grad_x = difference_pair(x_padded, 1, field.shape[1])[0]
    grad_z, curve_z = difference_pair(z_padded, 2, field.shape[2])
    transport = courant[0] * grad_x + courant[1] * grad_y + courant[2] * grad_z
    return field - transport + 0.05 * (curve_y + curve_z) + 0.3 * field / (1.0 + field * field)


def rows_below(values, stride, fill, sweep_direction):
    length = values.shape[sweep_direction]
    filler = jnp.full_like(lax.slice_in_dim(values, 0, stride, axis=sweep_direction), fill)
    return jnp.concatenate(
        [filler, lax.slice_in_dim(values, 0, length - stride, axis=sweep_direction)],
        sweep_direction,
    )


def rows_above(values, stride, fill, sweep_direction):
    length = values.shape[sweep_direction]
    filler = jnp.full_like(
        lax.slice_in_dim(values, length - stride, length, axis=sweep_direction), fill
    )
    return jnp.concatenate(
        [lax.slice_in_dim(values, stride, length, axis=sweep_direction), filler], sweep_direction
    )


def combine_rows(own_rows, below_set, above_set):
    lower_band, main_diagonal, upper_band, right_hand_sides = own_rows
    low_sub, low_diag, low_super, low_rights = below_set
    high_sub, high_diag, high_super, high_rights = above_set
    factor_low = -lower_band / low_diag
    factor_high = -upper_band / high_diag
    new_sub = factor_low * low_sub
    new_super = factor_high * high_super
    new_diag = main_diagonal + factor_low * low_super + factor_high * high_sub
    new_rights = tuple(
        (
            value + factor_low * lower_value + factor_high * upper_value
            for value, lower_value, upper_value in zip(right_hand_sides, low_rights, high_rights)
        )
    )
    return (new_sub, new_diag, new_super, new_rights)


def parallel_cyclic_reduction(
    lower_band, main_diagonal, upper_band, right_hand_sides, sweep_direction
):
    length = main_diagonal.shape[sweep_direction]
    stride = 1
    while stride < length:
        below_set = (
            rows_below(lower_band, stride, 0.0, sweep_direction),
            rows_below(main_diagonal, stride, 1.0, sweep_direction),
            rows_below(upper_band, stride, 0.0, sweep_direction),
            tuple((rows_below(value, stride, 0.0, sweep_direction) for value in right_hand_sides)),
        )
        above_set = (
            rows_above(lower_band, stride, 0.0, sweep_direction),
            rows_above(main_diagonal, stride, 1.0, sweep_direction),
            rows_above(upper_band, stride, 0.0, sweep_direction),
            tuple((rows_above(value, stride, 0.0, sweep_direction) for value in right_hand_sides)),
        )
        lower_band, main_diagonal, upper_band, right_hand_sides = combine_rows(
            (lower_band, main_diagonal, upper_band, right_hand_sides), below_set, above_set
        )
        stride = stride * 2
    return tuple((value / main_diagonal for value in right_hand_sides))


def to_chunks(values, chunks):
    planes, length, lanes = values.shape
    values = values.reshape(planes, chunks, length // chunks, lanes)
    return values.transpose(2, 1, 0, 3).reshape(length // chunks, chunks * planes, lanes)


def from_chunks(values, chunks):
    rows, sublanes, lanes = values.shape
    planes = sublanes // chunks
    values = values.reshape(rows, chunks, planes, lanes).transpose(2, 1, 0, 3)
    return values.reshape(planes, chunks * rows, lanes)


def thomas_kernel(rate_ref, right_ref, part_ref, first_ref, last_ref, ratio_ref):
    rows = rate_ref.shape[0]
    zero = jnp.zeros(rate_ref.shape[1:], jnp.float32)
    rate = rate_ref[1]
    inverse = 1.0 / (1.0 + 2.0 * rate)
    ratio = -rate * inverse
    part = right_ref[1] * inverse
    first = rate * inverse
    ratio_ref[1] = ratio
    part_ref[1] = part
    first_ref[1] = first

    def forward(i, carry):
        ratio, part, first, _ = carry
        rate = rate_ref[i]
        inverse = 1.0 / ((1.0 + 2.0 * rate) + rate * ratio)
        ratio = -rate * inverse
        part = (right_ref[i] + rate * part) * inverse
        first = rate * first * inverse
        ratio_ref[i] = ratio
        part_ref[i] = part
        first_ref[i] = first
        return ratio, part, first, inverse

    _, part, first, inverse = lax.fori_loop(
        2, rows - 1, forward, (ratio, part, first, zero), unroll=8
    )
    last = rate_ref[rows - 2] * inverse
    last_ref[rows - 2] = last

    def backward(j, carry):
        part, first, last = carry
        i = rows - 3 - j
        ratio = ratio_ref[i]
        part = part_ref[i] - ratio * part
        first = first_ref[i] - ratio * first
        last = -ratio * last
        part_ref[i] = part
        first_ref[i] = first
        last_ref[i] = last
        return part, first, last

    lax.fori_loop(0, rows - 3, backward, (part, first, last), unroll=8)
    for ref in (part_ref, first_ref, last_ref):
        ref[0] = zero
        ref[rows - 1] = zero


def local_solve(rate, right):
    shape = jax.ShapeDtypeStruct(rate.shape, jnp.float32)
    return pl.pallas_call(
        thomas_kernel,
        out_shape=(shape, shape, shape),
        scratch_shapes=[pltpu.VMEM(rate.shape, jnp.float32)],
    )(rate, right)


def shards(field, courant, diffusion_number):
    chunks = 2
    y_padded = padded_2(field, (("gy", 0),), 2, True)
    x_padded = padded_2(field, (("gx", 1),), 2, False)
    rhs = build_rhs(field, courant, y_padded, x_padded)
    place = lax.axis_index("gx")
    device_count = lax.axis_size("gx")
    planes = field.shape[0]
    rate = to_chunks(diffusion_number, chunks)
    right = to_chunks(rhs, chunks)
    part, first, last = local_solve(rate, right)
    rows = rate.shape[0]
    low_open = (place > 0).astype(jnp.float32)
    high_open = (place < device_count - 1).astype(jnp.float32)
    chunk_of = lax.broadcasted_iota(jnp.int32, (chunks, planes, 1), 0).reshape(chunks * planes, 1)
    low_scale = jnp.where(chunk_of == 0, low_open, 1.0)
    high_scale = jnp.where(chunk_of == chunks - 1, high_open, 1.0)
    rate_first, rate_last = rate[0], rate[rows - 1]
    sub_first = -rate_first * low_scale
    diag_first = (1.0 + 2.0 * rate_first) - rate_first * first[1]
    super_first = -rate_first * last[1]
    right_first = right[0] + rate_first * part[1]
    sub_last = -rate_last * first[rows - 2]
    diag_last = (1.0 + 2.0 * rate_last) - rate_last * last[rows - 2]
    super_last = -rate_last * high_scale
    right_last = right[rows - 1] + rate_last * part[rows - 2]
    stacked = jnp.stack(
        [sub_first, sub_last, diag_first, diag_last, super_first, super_last, right_first, right_last]
    )
    lanes = stacked.shape[-1]
    stacked = stacked.reshape(8, chunks, planes, lanes).transpose(2, 1, 0, 3)
    stacked = stacked.reshape(planes, chunks * 8, lanes)
    copies = jnp.broadcast_to(stacked[None], (device_count,) + stacked.shape)
    gathered = lax.all_to_all(copies, "gx", 0, 0, tiled=True)
    gathered = gathered.transpose(1, 0, 2, 3)
    gathered = gathered.reshape(planes, device_count, chunks, 4, 2, lanes)
    gathered_lower_band, gathered_diagonal, gathered_upper_band, gathered_rhs = (
        gathered[:, :, :, k].reshape(planes, 2 * chunks * device_count, lanes) for k in range(4)
    )
    boundary_rows_gathered = parallel_cyclic_reduction(
        gathered_lower_band, gathered_diagonal, gathered_upper_band, (gathered_rhs,), 1
    )[0]
    ends = lax.dynamic_slice_in_dim(boundary_rows_gathered, 2 * chunks * place, 2 * chunks, 1)
    ends = ends.reshape(planes, chunks, 2, lanes).transpose(2, 1, 0, 3)
    ends = ends.reshape(2, chunks * planes, lanes)
    start_value, end_value = ends[0], ends[1]
    solved = part + first * start_value[None] + last * end_value[None]
    row = lax.broadcasted_iota(jnp.int32, (rows, 1, 1), 0)
    solved = jnp.where(row == 0, start_value[None], solved)
    solved = jnp.where(row == rows - 1, end_value[None], solved)
    return from_chunks(solved, chunks)


def solution(mesh):
    in_specs = (P("gy", "gx", None), P(None, "gy", "gx", None), P("gy", "gx", None))
    out_specs = P("gy", "gx", None)
    return jax.shard_map(shards, mesh=mesh, in_specs=in_specs, out_specs=out_specs, check_vma=False)
```

```python
import jax
import jax.numpy as jnp
from jax import lax
from jax.sharding import PartitionSpec as P
from jax.experimental import pallas as pl
from jax.experimental.pallas import tpu as pltpu


def padded_2(cells, sides, width, closed):
    for axis, dim in sides:
        count = lax.axis_size(axis)
        ends = count if closed else count - 1
        head = lax.slice_in_dim(cells, 0, width, axis=dim)
        tail = lax.slice_in_dim(cells, cells.shape[dim] - width, cells.shape[dim], axis=dim)
        cells = jnp.concatenate(
            [
                lax.ppermute(tail, axis, [(i, (i + 1) % count) for i in range(ends)]),
                cells,
                lax.ppermute(head, axis, [((i + 1) % count, i) for i in range(ends)]),
            ],
            axis=dim,
        )
    return cells


def difference_pair(padded, sweep_direction, length):
    shifted = [
        lax.slice_in_dim(padded, offset, offset + length, axis=sweep_direction)
        for offset in range(5)
    ]
    gradient = (8.0 * (shifted[3] - shifted[1]) - (shifted[4] - shifted[0])) / 12.0
    curvature = (
        16.0 * (shifted[3] + shifted[1]) - (shifted[4] + shifted[0]) - 30.0 * shifted[2]
    ) / 12.0
    return (gradient, curvature)


def build_rhs(field, courant, y_padded, x_padded):
    z_padded = jnp.concatenate([field[:, :, -2:], field, field[:, :, :2]], 2)
    grad_y, curve_y = difference_pair(y_padded, 0, field.shape[0])
    grad_x = difference_pair(x_padded, 1, field.shape[1])[0]
    grad_z, curve_z = difference_pair(z_padded, 2, field.shape[2])
    transport = courant[0] * grad_x + courant[1] * grad_y + courant[2] * grad_z
    return field - transport + 0.05 * (curve_y + curve_z) + 0.3 * field / (1.0 + field * field)


def rows_below(values, stride, fill, sweep_direction):
    length = values.shape[sweep_direction]
    filler = jnp.full_like(lax.slice_in_dim(values, 0, stride, axis=sweep_direction), fill)
    return jnp.concatenate(
        [filler, lax.slice_in_dim(values, 0, length - stride, axis=sweep_direction)],
        sweep_direction,
    )


def rows_above(values, stride, fill, sweep_direction):
    length = values.shape[sweep_direction]
    filler = jnp.full_like(
        lax.slice_in_dim(values, length - stride, length, axis=sweep_direction), fill
    )
    return jnp.concatenate(
        [lax.slice_in_dim(values, stride, length, axis=sweep_direction), filler], sweep_direction
    )


def combine_rows(own_rows, below_set, above_set):
    lower_band, main_diagonal, upper_band, right_hand_sides = own_rows
    low_sub, low_diag, low_super, low_rights = below_set
    high_sub, high_diag, high_super, high_rights = above_set
    factor_low = -lower_band / low_diag
    factor_high = -upper_band / high_diag
    new_sub = factor_low * low_sub
    new_super = factor_high * high_super
    new_diag = main_diagonal + factor_low * low_super + factor_high * high_sub
    new_rights = tuple(
        (
            value + factor_low * lower_value + factor_high * upper_value
            for value, lower_value, upper_value in zip(right_hand_sides, low_rights, high_rights)
        )
    )
    return (new_sub, new_diag, new_super, new_rights)


def parallel_cyclic_reduction(
    lower_band, main_diagonal, upper_band, right_hand_sides, sweep_direction
):
    length = main_diagonal.shape[sweep_direction]
    stride = 1
    while stride < length:
        below_set = (
            rows_below(lower_band, stride, 0.0, sweep_direction),
            rows_below(main_diagonal, stride, 1.0, sweep_direction),
            rows_below(upper_band, stride, 0.0, sweep_direction),
            tuple((rows_below(value, stride, 0.0, sweep_direction) for value in right_hand_sides)),
        )
        above_set = (
            rows_above(lower_band, stride, 0.0, sweep_direction),
            rows_above(main_diagonal, stride, 1.0, sweep_direction),
            rows_above(upper_band, stride, 0.0, sweep_direction),
            tuple((rows_above(value, stride, 0.0, sweep_direction) for value in right_hand_sides)),
        )
        lower_band, main_diagonal, upper_band, right_hand_sides = combine_rows(
            (lower_band, main_diagonal, upper_band, right_hand_sides), below_set, above_set
        )
        stride = stride * 2
    return tuple((value / main_diagonal for value in right_hand_sides))


def to_chunks(values, chunks):
    planes, length, lanes = values.shape
    values = values.reshape(planes, chunks, length // chunks, lanes)
    return values.transpose(2, 1, 0, 3).reshape(length // chunks, chunks * planes, lanes)


def from_chunks(values, chunks):
    rows, sublanes, lanes = values.shape
    planes = sublanes // chunks
    values = values.reshape(rows, chunks, planes, lanes).transpose(2, 1, 0, 3)
    return values.reshape(planes, chunks * rows, lanes)


def thomas_kernel(rate_ref, right_ref, part_ref, first_ref, last_ref, ratio_ref):
    rows = rate_ref.shape[0]
    zero = jnp.zeros(rate_ref.shape[1:], jnp.float32)
    rate = rate_ref[1]
    inverse = 1.0 / (1.0 + 2.0 * rate)
    ratio = -rate * inverse
    part = right_ref[1] * inverse
    first = rate * inverse
    ratio_ref[1] = ratio
    part_ref[1] = part
    first_ref[1] = first

    def forward(i, carry):
        ratio, part, first, _ = carry
        rate = rate_ref[i]
        inverse = 1.0 / ((1.0 + 2.0 * rate) + rate * ratio)
        ratio = -rate * inverse
        part = (right_ref[i] + rate * part) * inverse
        first = rate * first * inverse
        ratio_ref[i] = ratio
        part_ref[i] = part
        first_ref[i] = first
        return ratio, part, first, inverse

    _, part, first, inverse = lax.fori_loop(
        2, rows - 1, forward, (ratio, part, first, zero), unroll=8
    )
    last = rate_ref[rows - 2] * inverse
    last_ref[rows - 2] = last

    def backward(j, carry):
        part, first, last = carry
        i = rows - 3 - j
        ratio = ratio_ref[i]
        part = part_ref[i] - ratio * part
        first = first_ref[i] - ratio * first
        last = -ratio * last
        part_ref[i] = part
        first_ref[i] = first
        last_ref[i] = last
        return part, first, last

    lax.fori_loop(0, rows - 3, backward, (part, first, last), unroll=8)
    for ref in (part_ref, first_ref, last_ref):
        ref[0] = zero
        ref[rows - 1] = zero


def local_solve(rate, right):
    shape = jax.ShapeDtypeStruct(rate.shape, jnp.float32)
    return pl.pallas_call(
        thomas_kernel,
        out_shape=(shape, shape, shape),
        scratch_shapes=[pltpu.VMEM(rate.shape, jnp.float32)],
    )(rate, right)


def shards(field, courant, diffusion_number):
    chunks = 2
    y_padded = padded_2(field, (("gy", 0),), 2, True)
    x_padded = jnp.pad(field, ((0, 0), (2, 2), (0, 0)))
    rhs = build_rhs(field, courant, y_padded, x_padded)
    place = lax.axis_index("gx")
    device_count = lax.axis_size("gx")
    planes, length, lanes = field.shape
    rate = to_chunks(diffusion_number, chunks)
    right = to_chunks(rhs, chunks)
    part, first, last = local_solve(rate, right)
    rows = rate.shape[0]
    low_open = (place > 0).astype(jnp.float32)
    high_open = (place < device_count - 1).astype(jnp.float32)
    chunk_of = lax.broadcasted_iota(jnp.int32, (chunks, planes, 1), 0).reshape(chunks * planes, 1)
    low_scale = jnp.where(chunk_of == 0, low_open, 1.0)
    high_scale = jnp.where(chunk_of == chunks - 1, high_open, 1.0)
    rate_first, rate_last = rate[0], rate[rows - 1]
    sub_first = -rate_first * low_scale
    diag_first = (1.0 + 2.0 * rate_first) - rate_first * first[1]
    super_first = -rate_first * last[1]
    right_first = right[0] + rate_first * part[1]
    sub_last = -rate_last * first[rows - 2]
    diag_last = (1.0 + 2.0 * rate_last) - rate_last * last[rows - 2]
    super_last = -rate_last * high_scale
    right_last = right[rows - 1] + rate_last * part[rows - 2]
    stacked = jnp.stack(
        [sub_first, sub_last, diag_first, diag_last, super_first, super_last, right_first, right_last]
    )
    stacked = stacked.reshape(8, chunks, planes, lanes).transpose(2, 1, 0, 3)
    stacked = stacked.reshape(planes, chunks * 8, lanes)
    speed = courant[0]
    lead_scale = speed[:, 1] / diffusion_number[:, 1]
    tail_scale = speed[:, length - 2] / diffusion_number[:, length - 2]
    lead_first = first[1, :planes] * rate_first[:planes]
    lead_last = first[rows - 2, :planes] * rate_last[:planes]
    tail_first = last[1, planes:] * rate_first[planes:]
    tail_last = last[rows - 2, planes:] * rate_last[planes:]
    extras = jnp.stack(
        [
            (8.0 * speed[:, 0] - lead_first * lead_scale) / 12.0,
            -speed[:, 0] / 12.0,
            -lead_last * lead_scale / 12.0,
            tail_first * tail_scale / 12.0,
            (tail_last * tail_scale - 8.0 * speed[:, length - 1]) / 12.0,
            speed[:, length - 1] / 12.0,
            field[:, 0],
            field[:, 1],
            field[:, length - 2],
            field[:, length - 1],
        ],
        1,
    )
    width = stacked.shape[1] + extras.shape[1]
    gathered = lax.all_gather(jnp.concatenate([stacked, extras], 1), "gx", axis=1, tiled=True)
    gathered = gathered.reshape(planes, device_count, width, lanes)
    extras = gathered[:, :, chunks * 8 :]
    gathered = gathered[:, :, : chunks * 8].reshape(planes, device_count, chunks, 4, 2, lanes)
    edge = jnp.zeros((planes, 1, lanes), jnp.float32)
    left_1 = jnp.concatenate([edge, extras[:, :-1, 9]], 1)
    left_2 = jnp.concatenate([edge, extras[:, :-1, 8]], 1)
    right_1 = jnp.concatenate([extras[:, 1:, 6], edge], 1)
    right_2 = jnp.concatenate([extras[:, 1:, 7], edge], 1)
    correction = jnp.stack(
        [
            extras[:, :, 0] * left_1 + extras[:, :, 1] * left_2,
            extras[:, :, 2] * left_1,
            extras[:, :, 3] * right_1,
            extras[:, :, 4] * right_1 + extras[:, :, 5] * right_2,
        ],
        2,
    ).reshape(planes, device_count, chunks, 2, lanes)
    gathered_lower_band, gathered_diagonal, gathered_upper_band, gathered_rhs = (
        gathered[:, :, :, k].reshape(planes, 2 * chunks * device_count, lanes) for k in range(4)
    )
    gathered_rhs = (gathered[:, :, :, 3] + correction).reshape(planes, 2 * chunks * device_count, lanes)
    boundary_rows_gathered = parallel_cyclic_reduction(
        gathered_lower_band, gathered_diagonal, gathered_upper_band, (gathered_rhs,), 1
    )[0]
    ends = lax.dynamic_slice_in_dim(boundary_rows_gathered, 2 * chunks * place, 2 * chunks, 1)
    ends = ends.reshape(planes, chunks, 2, lanes).transpose(2, 1, 0, 3)
    ends = ends.reshape(2, chunks * planes, lanes)
    own_left = lax.dynamic_slice_in_dim(left_1, place, 1, 1)[:, 0]
    own_right = lax.dynamic_slice_in_dim(right_1, place, 1, 1)[:, 0]
    lead_shift = -lead_scale * own_left / 12.0
    tail_shift = tail_scale * own_right / 12.0
    zero = jnp.zeros_like(lead_shift)
    lead_shift = jnp.concatenate([lead_shift, zero], 0)
    tail_shift = jnp.concatenate([zero, tail_shift], 0)
    start_value, end_value = ends[0], ends[1]
    solved = part + first * (start_value + lead_shift)[None] + last * (end_value + tail_shift)[None]
    row = lax.broadcasted_iota(jnp.int32, (rows, 1, 1), 0)
    solved = jnp.where(row == 0, start_value[None], solved)
    solved = jnp.where(row == rows - 1, end_value[None], solved)
    return from_chunks(solved, chunks)


def solution(mesh):
    in_specs = (P("gy", "gx", None), P(None, "gy", "gx", None), P("gy", "gx", None))
    out_specs = P("gy", "gx", None)
    return jax.shard_map(shards, mesh=mesh, in_specs=in_specs, out_specs=out_specs, check_vma=False)
```

```python
import jax
import jax.numpy as jnp
from jax import lax
from jax.sharding import PartitionSpec as P
from jax.experimental import pallas as pl
from jax.experimental.pallas import tpu as pltpu


def padded_2(cells, sides, width, closed):
    for axis, dim in sides:
        count = lax.axis_size(axis)
        ends = count if closed else count - 1
        head = lax.slice_in_dim(cells, 0, width, axis=dim)
        tail = lax.slice_in_dim(cells, cells.shape[dim] - width, cells.shape[dim], axis=dim)
        cells = jnp.concatenate(
            [
                lax.ppermute(tail, axis, [(i, (i + 1) % count) for i in range(ends)]),
                cells,
                lax.ppermute(head, axis, [((i + 1) % count, i) for i in range(ends)]),
            ],
            axis=dim,
        )
    return cells


def difference_pair(padded, sweep_direction, length):
    shifted = [
        lax.slice_in_dim(padded, offset, offset + length, axis=sweep_direction)
        for offset in range(5)
    ]
    gradient = (8.0 * (shifted[3] - shifted[1]) - (shifted[4] - shifted[0])) / 12.0
    curvature = (
        16.0 * (shifted[3] + shifted[1]) - (shifted[4] + shifted[0]) - 30.0 * shifted[2]
    ) / 12.0
    return (gradient, curvature)


def build_rhs(field, courant, y_padded, x_padded):
    z_padded = jnp.concatenate([field[:, :, -2:], field, field[:, :, :2]], 2)
    grad_y, curve_y = difference_pair(y_padded, 0, field.shape[0])
    grad_x = difference_pair(x_padded, 1, field.shape[1])[0]
    grad_z, curve_z = difference_pair(z_padded, 2, field.shape[2])
    transport = courant[0] * grad_x + courant[1] * grad_y + courant[2] * grad_z
    return field - transport + 0.05 * (curve_y + curve_z) + 0.3 * field / (1.0 + field * field)


def rows_below(values, stride, fill, sweep_direction):
    length = values.shape[sweep_direction]
    filler = jnp.full_like(lax.slice_in_dim(values, 0, stride, axis=sweep_direction), fill)
    return jnp.concatenate(
        [filler, lax.slice_in_dim(values, 0, length - stride, axis=sweep_direction)],
        sweep_direction,
    )


def rows_above(values, stride, fill, sweep_direction):
    length = values.shape[sweep_direction]
    filler = jnp.full_like(
        lax.slice_in_dim(values, length - stride, length, axis=sweep_direction), fill
    )
    return jnp.concatenate(
        [lax.slice_in_dim(values, stride, length, axis=sweep_direction), filler], sweep_direction
    )


def combine_rows(own_rows, below_set, above_set):
    lower_band, main_diagonal, upper_band, right_hand_sides = own_rows
    low_sub, low_diag, low_super, low_rights = below_set
    high_sub, high_diag, high_super, high_rights = above_set
    factor_low = -lower_band / low_diag
    factor_high = -upper_band / high_diag
    new_sub = factor_low * low_sub
    new_super = factor_high * high_super
    new_diag = main_diagonal + factor_low * low_super + factor_high * high_sub
    new_rights = tuple(
        (
            value + factor_low * lower_value + factor_high * upper_value
            for value, lower_value, upper_value in zip(right_hand_sides, low_rights, high_rights)
        )
    )
    return (new_sub, new_diag, new_super, new_rights)


def parallel_cyclic_reduction(
    lower_band, main_diagonal, upper_band, right_hand_sides, sweep_direction
):
    length = main_diagonal.shape[sweep_direction]
    stride = 1
    while stride < length:
        below_set = (
            rows_below(lower_band, stride, 0.0, sweep_direction),
            rows_below(main_diagonal, stride, 1.0, sweep_direction),
            rows_below(upper_band, stride, 0.0, sweep_direction),
            tuple((rows_below(value, stride, 0.0, sweep_direction) for value in right_hand_sides)),
        )
        above_set = (
            rows_above(lower_band, stride, 0.0, sweep_direction),
            rows_above(main_diagonal, stride, 1.0, sweep_direction),
            rows_above(upper_band, stride, 0.0, sweep_direction),
            tuple((rows_above(value, stride, 0.0, sweep_direction) for value in right_hand_sides)),
        )
        lower_band, main_diagonal, upper_band, right_hand_sides = combine_rows(
            (lower_band, main_diagonal, upper_band, right_hand_sides), below_set, above_set
        )
        stride = stride * 2
    return tuple((value / main_diagonal for value in right_hand_sides))


def to_chunks(values, chunks):
    planes, length, lanes = values.shape
    values = values.reshape(planes, chunks, length // chunks, lanes)
    return values.transpose(2, 1, 0, 3).reshape(length // chunks, chunks * planes, lanes)


def from_chunks(values, chunks):
    rows, sublanes, lanes = values.shape
    planes = sublanes // chunks
    values = values.reshape(rows, chunks, planes, lanes).transpose(2, 1, 0, 3)
    return values.reshape(planes, chunks * rows, lanes)


def factor_kernel(rate_ref, ratio_ref, inverse_ref, first_ref, last_ref):
    rows = rate_ref.shape[0]
    zero = jnp.zeros(rate_ref.shape[1:], jnp.float32)
    rate = rate_ref[1]
    inverse = 1.0 / (1.0 + 2.0 * rate)
    ratio = -rate * inverse
    first = rate * inverse
    ratio_ref[1] = ratio
    inverse_ref[1] = inverse
    first_ref[1] = first

    def forward(i, carry):
        ratio, first, _ = carry
        rate = rate_ref[i]
        inverse = 1.0 / ((1.0 + 2.0 * rate) + rate * ratio)
        ratio = -rate * inverse
        first = rate * first * inverse
        ratio_ref[i] = ratio
        inverse_ref[i] = inverse
        first_ref[i] = first
        return ratio, first, inverse

    _, first, inverse = lax.fori_loop(2, rows - 1, forward, (ratio, first, zero), unroll=8)
    last = rate_ref[rows - 2] * inverse
    last_ref[rows - 2] = last

    def backward(j, carry):
        first, last = carry
        i = rows - 3 - j
        ratio = ratio_ref[i]
        first = first_ref[i] - ratio * first
        last = -ratio * last
        first_ref[i] = first
        last_ref[i] = last
        return first, last

    lax.fori_loop(0, rows - 3, backward, (first, last), unroll=8)
    for ref in (ratio_ref, inverse_ref, first_ref, last_ref):
        ref[0] = zero
        ref[rows - 1] = zero


def substitute_kernel(rate_ref, ratio_ref, inverse_ref, right_ref, part_ref):
    rows = rate_ref.shape[0]
    zero = jnp.zeros(rate_ref.shape[1:], jnp.float32)
    part = right_ref[1] * inverse_ref[1]
    part_ref[1] = part

    def forward(i, part):
        part = (right_ref[i] + rate_ref[i] * part) * inverse_ref[i]
        part_ref[i] = part
        return part

    part = lax.fori_loop(2, rows - 1, forward, part, unroll=8)

    def backward(j, part):
        i = rows - 3 - j
        part = part_ref[i] - ratio_ref[i] * part
        part_ref[i] = part
        return part

    lax.fori_loop(0, rows - 3, backward, part, unroll=8)
    part_ref[0] = zero
    part_ref[rows - 1] = zero


def local_factor(rate):
    shape = jax.ShapeDtypeStruct(rate.shape, jnp.float32)
    return pl.pallas_call(factor_kernel, out_shape=(shape,) * 4)(rate)


def local_substitute(rate, ratio, inverse, right):
    shape = jax.ShapeDtypeStruct(rate.shape, jnp.float32)
    return pl.pallas_call(substitute_kernel, out_shape=shape)(rate, ratio, inverse, right)


def shards(field, courant, diffusion_number):
    chunks = 2
    y_padded = padded_2(field, (("gy", 0),), 2, True)
    x_padded = padded_2(field, (("gx", 1),), 2, False)
    flat = jnp.zeros_like(field[:2])
    own_rhs = build_rhs(field, courant, jnp.concatenate([flat, field, flat], 0), x_padded)
    own_rhs = lax.optimization_barrier(own_rhs)
    halo_only = jnp.concatenate([y_padded[:2], jnp.zeros_like(field), y_padded[-2:]], 0)
    grad_y, curve_y = difference_pair(halo_only, 0, field.shape[0])
    rhs = own_rhs + (0.05 * curve_y - courant[1] * grad_y)
    place = lax.axis_index("gx")
    device_count = lax.axis_size("gx")
    planes = field.shape[0]
    rate = to_chunks(diffusion_number, chunks)
    right = to_chunks(rhs, chunks)
    ratio, inverse, first, last = local_factor(rate)
    part = local_substitute(rate, ratio, inverse, right)
    rows = rate.shape[0]
    low_open = (place > 0).astype(jnp.float32)
    high_open = (place < device_count - 1).astype(jnp.float32)
    chunk_of = lax.broadcasted_iota(jnp.int32, (chunks, planes, 1), 0).reshape(chunks * planes, 1)
    low_scale = jnp.where(chunk_of == 0, low_open, 1.0)
    high_scale = jnp.where(chunk_of == chunks - 1, high_open, 1.0)
    rate_first, rate_last = rate[0], rate[rows - 1]
    sub_first = -rate_first * low_scale
    diag_first = (1.0 + 2.0 * rate_first) - rate_first * first[1]
    super_first = -rate_first * last[1]
    right_first = right[0] + rate_first * part[1]
    sub_last = -rate_last * first[rows - 2]
    diag_last = (1.0 + 2.0 * rate_last) - rate_last * last[rows - 2]
    super_last = -rate_last * high_scale
    right_last = right[rows - 1] + rate_last * part[rows - 2]
    stacked = jnp.stack(
        [sub_first, sub_last, diag_first, diag_last, super_first, super_last, right_first, right_last]
    )
    lanes = stacked.shape[-1]
    stacked = stacked.reshape(8, chunks, planes, lanes).transpose(2, 1, 0, 3)
    stacked = stacked.reshape(planes, chunks * 8, lanes)
    gathered = lax.all_gather(stacked, "gx", axis=1, tiled=True)
    gathered = gathered.reshape(planes, device_count, chunks, 4, 2, lanes)
    gathered_lower_band, gathered_diagonal, gathered_upper_band, gathered_rhs = (
        gathered[:, :, :, k].reshape(planes, 2 * chunks * device_count, lanes) for k in range(4)
    )
    boundary_rows_gathered = parallel_cyclic_reduction(
        gathered_lower_band, gathered_diagonal, gathered_upper_band, (gathered_rhs,), 1
    )[0]
    ends = lax.dynamic_slice_in_dim(boundary_rows_gathered, 2 * chunks * place, 2 * chunks, 1)
    ends = ends.reshape(planes, chunks, 2, lanes).transpose(2, 1, 0, 3)
    ends = ends.reshape(2, chunks * planes, lanes)
    start_value, end_value = ends[0], ends[1]
    solved = part + first * start_value[None] + last * end_value[None]
    row = lax.broadcasted_iota(jnp.int32, (rows, 1, 1), 0)
    solved = jnp.where(row == 0, start_value[None], solved)
    solved = jnp.where(row == rows - 1, end_value[None], solved)
    return from_chunks(solved, chunks)


def solution(mesh):
    in_specs = (P("gy", "gx", None), P(None, "gy", "gx", None), P("gy", "gx", None))
    out_specs = P("gy", "gx", None)
    return jax.shard_map(shards, mesh=mesh, in_specs=in_specs, out_specs=out_specs, check_vma=False)
```

```python
import jax
import jax.numpy as jnp
from jax import lax
from jax.sharding import PartitionSpec as P
from jax.experimental import pallas as pl
from jax.experimental.pallas import tpu as pltpu


def padded_2(cells, sides, width, closed):
    for axis, dim in sides:
        count = lax.axis_size(axis)
        ends = count if closed else count - 1
        head = lax.slice_in_dim(cells, 0, width, axis=dim)
        tail = lax.slice_in_dim(cells, cells.shape[dim] - width, cells.shape[dim], axis=dim)
        cells = jnp.concatenate(
            [
                lax.ppermute(tail, axis, [(i, (i + 1) % count) for i in range(ends)]),
                cells,
                lax.ppermute(head, axis, [((i + 1) % count, i) for i in range(ends)]),
            ],
            axis=dim,
        )
    return cells


def difference_pair(padded, sweep_direction, length):
    shifted = [
        lax.slice_in_dim(padded, offset, offset + length, axis=sweep_direction)
        for offset in range(5)
    ]
    gradient = (8.0 * (shifted[3] - shifted[1]) - (shifted[4] - shifted[0])) / 12.0
    curvature = (
        16.0 * (shifted[3] + shifted[1]) - (shifted[4] + shifted[0]) - 30.0 * shifted[2]
    ) / 12.0
    return (gradient, curvature)


def build_rhs(field, courant, y_padded, x_padded):
    z_padded = jnp.concatenate([field[:, :, -2:], field, field[:, :, :2]], 2)
    grad_y, curve_y = difference_pair(y_padded, 0, field.shape[0])
    grad_x = difference_pair(x_padded, 1, field.shape[1])[0]
    grad_z, curve_z = difference_pair(z_padded, 2, field.shape[2])
    transport = courant[0] * grad_x + courant[1] * grad_y + courant[2] * grad_z
    return field - transport + 0.05 * (curve_y + curve_z) + 0.3 * field / (1.0 + field * field)


def rows_below(values, stride, fill, sweep_direction):
    length = values.shape[sweep_direction]
    filler = jnp.full_like(lax.slice_in_dim(values, 0, stride, axis=sweep_direction), fill)
    return jnp.concatenate(
        [filler, lax.slice_in_dim(values, 0, length - stride, axis=sweep_direction)],
        sweep_direction,
    )


def rows_above(values, stride, fill, sweep_direction):
    length = values.shape[sweep_direction]
    filler = jnp.full_like(
        lax.slice_in_dim(values, length - stride, length, axis=sweep_direction), fill
    )
    return jnp.concatenate(
        [lax.slice_in_dim(values, stride, length, axis=sweep_direction), filler], sweep_direction
    )


def combine_rows(own_rows, below_set, above_set):
    lower_band, main_diagonal, upper_band, right_hand_sides = own_rows
    low_sub, low_diag, low_super, low_rights = below_set
    high_sub, high_diag, high_super, high_rights = above_set
    factor_low = -lower_band / low_diag
    factor_high = -upper_band / high_diag
    new_sub = factor_low * low_sub
    new_super = factor_high * high_super
    new_diag = main_diagonal + factor_low * low_super + factor_high * high_sub
    new_rights = tuple(
        (
            value + factor_low * lower_value + factor_high * upper_value
            for value, lower_value, upper_value in zip(right_hand_sides, low_rights, high_rights)
        )
    )
    return (new_sub, new_diag, new_super, new_rights)


def parallel_cyclic_reduction(
    lower_band, main_diagonal, upper_band, right_hand_sides, sweep_direction
):
    length = main_diagonal.shape[sweep_direction]
    stride = 1
    while stride < length:
        below_set = (
            rows_below(lower_band, stride, 0.0, sweep_direction),
            rows_below(main_diagonal, stride, 1.0, sweep_direction),
            rows_below(upper_band, stride, 0.0, sweep_direction),
            tuple((rows_below(value, stride, 0.0, sweep_direction) for value in right_hand_sides)),
        )
        above_set = (
            rows_above(lower_band, stride, 0.0, sweep_direction),
            rows_above(main_diagonal, stride, 1.0, sweep_direction),
            rows_above(upper_band, stride, 0.0, sweep_direction),
            tuple((rows_above(value, stride, 0.0, sweep_direction) for value in right_hand_sides)),
        )
        lower_band, main_diagonal, upper_band, right_hand_sides = combine_rows(
            (lower_band, main_diagonal, upper_band, right_hand_sides), below_set, above_set
        )
        stride = stride * 2
    return tuple((value / main_diagonal for value in right_hand_sides))


def thomas_kernel(rate_ref, right_ref, part_ref, first_ref, last_ref, ratio_ref, ahead_ref, lead_ref):
    rows = ratio_ref.shape[0]
    sublanes = ratio_ref.shape[1]

    def at(i):
        return pl.ds(i, sublanes, stride=rows)

    zero = jnp.zeros(ratio_ref.shape[1:], jnp.float32)
    rate = rate_ref[at(1)]
    inverse = 1.0 / (1.0 + 2.0 * rate)
    ratio = -rate * inverse
    part = right_ref[at(1)] * inverse
    first = rate * inverse
    ratio_ref[1] = ratio
    ahead_ref[1] = part
    lead_ref[1] = first

    def forward(i, carry):
        ratio, part, first, _ = carry
        rate = rate_ref[at(i)]
        inverse = 1.0 / ((1.0 + 2.0 * rate) + rate * ratio)
        ratio = -rate * inverse
        part = (right_ref[at(i)] + rate * part) * inverse
        first = rate * first * inverse
        ratio_ref[i] = ratio
        ahead_ref[i] = part
        lead_ref[i] = first
        return ratio, part, first, inverse

    _, part, first, inverse = lax.fori_loop(
        2, rows - 1, forward, (ratio, part, first, zero), unroll=8
    )
    last = rate_ref[at(rows - 2)] * inverse
    part_ref[at(rows - 2)] = part
    first_ref[at(rows - 2)] = first
    last_ref[at(rows - 2)] = last

    def backward(j, carry):
        part, first, last = carry
        i = rows - 3 - j
        ratio = ratio_ref[i]
        part = ahead_ref[i] - ratio * part
        first = lead_ref[i] - ratio * first
        last = -ratio * last
        part_ref[at(i)] = part
        first_ref[at(i)] = first
        last_ref[at(i)] = last
        return part, first, last

    lax.fori_loop(0, rows - 3, backward, (part, first, last), unroll=8)
    for ref in (part_ref, first_ref, last_ref):
        ref[at(0)] = zero
        ref[at(rows - 1)] = zero


def local_solve(rate, right, chunks):
    planes, length, lanes = rate.shape
    rows = length // chunks
    flat = jax.ShapeDtypeStruct((planes * length, lanes), jnp.float32)
    scratch = pltpu.VMEM((rows, planes * chunks, lanes), jnp.float32)
    outs = pl.pallas_call(
        thomas_kernel,
        out_shape=(flat, flat, flat),
        scratch_shapes=[scratch, scratch, scratch],
    )(rate.reshape(planes * length, lanes), right.reshape(planes * length, lanes))
    return tuple(out.reshape(planes, chunks, rows, lanes) for out in outs)


def shards(field, courant, diffusion_number):
    chunks = 2
    y_padded = padded_2(field, (("gy", 0),), 2, True)
    x_padded = padded_2(field, (("gx", 1),), 2, False)
    rhs = build_rhs(field, courant, y_padded, x_padded)
    place = lax.axis_index("gx")
    device_count = lax.axis_size("gx")
    planes = field.shape[0]
    part, first, last = local_solve(diffusion_number, rhs, chunks)
    rows = part.shape[2]
    rate = diffusion_number.reshape(planes, chunks, rows, -1)
    right = rhs.reshape(planes, chunks, rows, -1)
    low_open = (place > 0).astype(jnp.float32)
    high_open = (place < device_count - 1).astype(jnp.float32)
    chunk_of = lax.broadcasted_iota(jnp.int32, (1, chunks, 1), 1)
    low_scale = jnp.where(chunk_of == 0, low_open, 1.0)
    high_scale = jnp.where(chunk_of == chunks - 1, high_open, 1.0)
    rate_first, rate_last = rate[:, :, 0], rate[:, :, rows - 1]
    sub_first = -rate_first * low_scale
    diag_first = (1.0 + 2.0 * rate_first) - rate_first * first[:, :, 1]
    super_first = -rate_first * last[:, :, 1]
    right_first = right[:, :, 0] + rate_first * part[:, :, 1]
    sub_last = -rate_last * first[:, :, rows - 2]
    diag_last = (1.0 + 2.0 * rate_last) - rate_last * last[:, :, rows - 2]
    super_last = -rate_last * high_scale
    right_last = right[:, :, rows - 1] + rate_last * part[:, :, rows - 2]
    stacked = jnp.stack(
        [sub_first, sub_last, diag_first, diag_last, super_first, super_last, right_first, right_last], 2
    )
    lanes = stacked.shape[-1]
    stacked = stacked.reshape(planes, chunks * 8, lanes)
    gathered = lax.all_gather(stacked, "gx", axis=1, tiled=True)
    gathered = gathered.reshape(planes, device_count, chunks, 4, 2, lanes)
    gathered_lower_band, gathered_diagonal, gathered_upper_band, gathered_rhs = (
        gathered[:, :, :, k].reshape(planes, 2 * chunks * device_count, lanes) for k in range(4)
    )
    boundary_rows_gathered = parallel_cyclic_reduction(
        gathered_lower_band, gathered_diagonal, gathered_upper_band, (gathered_rhs,), 1
    )[0]
    ends = lax.dynamic_slice_in_dim(boundary_rows_gathered, 2 * chunks * place, 2 * chunks, 1)
    ends = ends.reshape(planes, chunks, 2, 1, lanes)
    start_value, end_value = ends[:, :, 0], ends[:, :, 1]
    solved = part + first * start_value + last * end_value
    row = lax.broadcasted_iota(jnp.int32, (1, 1, rows, 1), 2)
    solved = jnp.where(row == 0, start_value, solved)
    solved = jnp.where(row == rows - 1, end_value, solved)
    return solved.reshape(planes, chunks * rows, lanes)


def solution(mesh):
    in_specs = (P("gy", "gx", None), P(None, "gy", "gx", None), P("gy", "gx", None))
    out_specs = P("gy", "gx", None)
    return jax.shard_map(shards, mesh=mesh, in_specs=in_specs, out_specs=out_specs, check_vma=False)
```

```python
import jax
import jax.numpy as jnp
from jax import lax
from jax.sharding import PartitionSpec as P
from jax.experimental import pallas as pl
from jax.experimental.pallas import tpu as pltpu


def padded_2(cells, sides, width, closed):
    for axis, dim in sides:
        count = lax.axis_size(axis)
        ends = count if closed else count - 1
        head = lax.slice_in_dim(cells, 0, width, axis=dim)
        tail = lax.slice_in_dim(cells, cells.shape[dim] - width, cells.shape[dim], axis=dim)
        cells = jnp.concatenate(
            [
                lax.ppermute(tail, axis, [(i, (i + 1) % count) for i in range(ends)]),
                cells,
                lax.ppermute(head, axis, [((i + 1) % count, i) for i in range(ends)]),
            ],
            axis=dim,
        )
    return cells


def difference_pair(padded, sweep_direction, length):
    shifted = [
        lax.slice_in_dim(padded, offset, offset + length, axis=sweep_direction)
        for offset in range(5)
    ]
    gradient = (8.0 * (shifted[3] - shifted[1]) - (shifted[4] - shifted[0])) / 12.0
    curvature = (
        16.0 * (shifted[3] + shifted[1]) - (shifted[4] + shifted[0]) - 30.0 * shifted[2]
    ) / 12.0
    return (gradient, curvature)


def build_rhs(field, courant, y_padded, x_padded):
    z_padded = jnp.concatenate([field[:, :, -2:], field, field[:, :, :2]], 2)
    grad_y, curve_y = difference_pair(y_padded, 0, field.shape[0])
    grad_x = difference_pair(x_padded, 1, field.shape[1])[0]
    grad_z, curve_z = difference_pair(z_padded, 2, field.shape[2])
    transport = courant[0] * grad_x + courant[1] * grad_y + courant[2] * grad_z
    return field - transport + 0.05 * (curve_y + curve_z) + 0.3 * field / (1.0 + field * field)


def rows_below(values, stride, fill, sweep_direction):
    length = values.shape[sweep_direction]
    filler = jnp.full_like(lax.slice_in_dim(values, 0, stride, axis=sweep_direction), fill)
    return jnp.concatenate(
        [filler, lax.slice_in_dim(values, 0, length - stride, axis=sweep_direction)],
        sweep_direction,
    )


def rows_above(values, stride, fill, sweep_direction):
    length = values.shape[sweep_direction]
    filler = jnp.full_like(
        lax.slice_in_dim(values, length - stride, length, axis=sweep_direction), fill
    )
    return jnp.concatenate(
        [lax.slice_in_dim(values, stride, length, axis=sweep_direction), filler], sweep_direction
    )


def combine_rows(own_rows, below_set, above_set):
    lower_band, main_diagonal, upper_band, right_hand_sides = own_rows
    low_sub, low_diag, low_super, low_rights = below_set
    high_sub, high_diag, high_super, high_rights = above_set
    factor_low = -lower_band / low_diag
    factor_high = -upper_band / high_diag
    new_sub = factor_low * low_sub
    new_super = factor_high * high_super
    new_diag = main_diagonal + factor_low * low_super + factor_high * high_sub
    new_rights = tuple(
        (
            value + factor_low * lower_value + factor_high * upper_value
            for value, lower_value, upper_value in zip(right_hand_sides, low_rights, high_rights)
        )
    )
    return (new_sub, new_diag, new_super, new_rights)


def parallel_cyclic_reduction(
    lower_band, main_diagonal, upper_band, right_hand_sides, sweep_direction
):
    length = main_diagonal.shape[sweep_direction]
    stride = 1
    while stride < length:
        below_set = (
            rows_below(lower_band, stride, 0.0, sweep_direction),
            rows_below(main_diagonal, stride, 1.0, sweep_direction),
            rows_below(upper_band, stride, 0.0, sweep_direction),
            tuple((rows_below(value, stride, 0.0, sweep_direction) for value in right_hand_sides)),
        )
        above_set = (
            rows_above(lower_band, stride, 0.0, sweep_direction),
            rows_above(main_diagonal, stride, 1.0, sweep_direction),
            rows_above(upper_band, stride, 0.0, sweep_direction),
            tuple((rows_above(value, stride, 0.0, sweep_direction) for value in right_hand_sides)),
        )
        lower_band, main_diagonal, upper_band, right_hand_sides = combine_rows(
            (lower_band, main_diagonal, upper_band, right_hand_sides), below_set, above_set
        )
        stride = stride * 2
    return tuple((value / main_diagonal for value in right_hand_sides))


def thomas_kernel(rate_ref, right_ref, part_ref, first_ref, last_ref, ratio_ref, ahead_ref, lead_ref):
    rows = ratio_ref.shape[0]
    sublanes = ratio_ref.shape[1]

    def at(i):
        return pl.ds(i, sublanes, stride=rows)

    zero = jnp.zeros(ratio_ref.shape[1:], jnp.float32)
    rate = rate_ref[at(1)]
    inverse = 1.0 / (1.0 + 2.0 * rate)
    ratio = -rate * inverse
    part = right_ref[at(1)] * inverse
    first = rate * inverse
    ratio_ref[1] = ratio
    ahead_ref[1] = part
    lead_ref[1] = first

    def forward(i, carry):
        ratio, part, first, _ = carry
        rate = rate_ref[at(i)]
        inverse = 1.0 / ((1.0 + 2.0 * rate) + rate * ratio)
        ratio = -rate * inverse
        part = (right_ref[at(i)] + rate * part) * inverse
        first = rate * first * inverse
        ratio_ref[i] = ratio
        ahead_ref[i] = part
        lead_ref[i] = first
        return ratio, part, first, inverse

    _, part, first, inverse = lax.fori_loop(
        2, rows - 1, forward, (ratio, part, first, zero), unroll=8
    )
    last = rate_ref[at(rows - 2)] * inverse
    part_ref[at(rows - 2)] = part
    first_ref[at(rows - 2)] = first
    last_ref[at(rows - 2)] = last

    def backward(j, carry):
        part, first, last = carry
        i = rows - 3 - j
        ratio = ratio_ref[i]
        part = ahead_ref[i] - ratio * part
        first = lead_ref[i] - ratio * first
        last = -ratio * last
        part_ref[at(i)] = part
        first_ref[at(i)] = first
        last_ref[at(i)] = last
        return part, first, last

    lax.fori_loop(0, rows - 3, backward, (part, first, last), unroll=8)
    for ref in (part_ref, first_ref, last_ref):
        ref[at(0)] = zero
        ref[at(rows - 1)] = zero


def local_solve(rate, right, chunks):
    planes, length, lanes = rate.shape
    rows = length // chunks
    flat = jax.ShapeDtypeStruct((planes * length, lanes), jnp.float32)
    scratch = pltpu.VMEM((rows, planes * chunks, lanes), jnp.float32)
    outs = pl.pallas_call(
        thomas_kernel,
        out_shape=(flat, flat, flat),
        scratch_shapes=[scratch, scratch, scratch],
    )(rate.reshape(planes * length, lanes), right.reshape(planes * length, lanes))
    return tuple(out.reshape(planes, chunks, rows, lanes) for out in outs)


def shards(field, courant, diffusion_number):
    chunks = 4
    y_padded = padded_2(field, (("gy", 0),), 2, True)
    x_padded = padded_2(field, (("gx", 1),), 2, False)
    rhs = build_rhs(field, courant, y_padded, x_padded)
    place = lax.axis_index("gx")
    device_count = lax.axis_size("gx")
    planes = field.shape[0]
    part, first, last = local_solve(diffusion_number, rhs, chunks)
    rows = part.shape[2]
    rate = diffusion_number.reshape(planes, chunks, rows, -1)
    right = rhs.reshape(planes, chunks, rows, -1)
    low_open = (place > 0).astype(jnp.float32)
    high_open = (place < device_count - 1).astype(jnp.float32)
    chunk_of = lax.broadcasted_iota(jnp.int32, (1, chunks, 1), 1)
    low_scale = jnp.where(chunk_of == 0, low_open, 1.0)
    high_scale = jnp.where(chunk_of == chunks - 1, high_open, 1.0)
    rate_first, rate_last = rate[:, :, 0], rate[:, :, rows - 1]
    sub_first = -rate_first * low_scale
    diag_first = (1.0 + 2.0 * rate_first) - rate_first * first[:, :, 1]
    super_first = -rate_first * last[:, :, 1]
    right_first = right[:, :, 0] + rate_first * part[:, :, 1]
    sub_last = -rate_last * first[:, :, rows - 2]
    diag_last = (1.0 + 2.0 * rate_last) - rate_last * last[:, :, rows - 2]
    super_last = -rate_last * high_scale
    right_last = right[:, :, rows - 1] + rate_last * part[:, :, rows - 2]
    stacked = jnp.stack(
        [sub_first, sub_last, diag_first, diag_last, super_first, super_last, right_first, right_last], 2
    )
    lanes = stacked.shape[-1]
    stacked = stacked.reshape(planes, chunks * 8, lanes)
    gathered = lax.all_gather(stacked, "gx", axis=1, tiled=True)
    gathered = gathered.reshape(planes, device_count, chunks, 4, 2, lanes)
    gathered_lower_band, gathered_diagonal, gathered_upper_band, gathered_rhs = (
        gathered[:, :, :, k].reshape(planes, 2 * chunks * device_count, lanes) for k in range(4)
    )
    boundary_rows_gathered = parallel_cyclic_reduction(
        gathered_lower_band, gathered_diagonal, gathered_upper_band, (gathered_rhs,), 1
    )[0]
    ends = lax.dynamic_slice_in_dim(boundary_rows_gathered, 2 * chunks * place, 2 * chunks, 1)
    ends = ends.reshape(planes, chunks, 2, 1, lanes)
    start_value, end_value = ends[:, :, 0], ends[:, :, 1]
    solved = part + first * start_value + last * end_value
    row = lax.broadcasted_iota(jnp.int32, (1, 1, rows, 1), 2)
    solved = jnp.where(row == 0, start_value, solved)
    solved = jnp.where(row == rows - 1, end_value, solved)
    return solved.reshape(planes, chunks * rows, lanes)


def solution(mesh):
    in_specs = (P("gy", "gx", None), P(None, "gy", "gx", None), P("gy", "gx", None))
    out_specs = P("gy", "gx", None)
    return jax.shard_map(shards, mesh=mesh, in_specs=in_specs, out_specs=out_specs, check_vma=False)
```

```python
import jax
import jax.numpy as jnp
from jax import lax
from jax.sharding import PartitionSpec as P
from jax.experimental import pallas as pl
from jax.experimental.pallas import tpu as pltpu


def padded_2(cells, sides, width, closed):
    for axis, dim in sides:
        count = lax.axis_size(axis)
        ends = count if closed else count - 1
        head = lax.slice_in_dim(cells, 0, width, axis=dim)
        tail = lax.slice_in_dim(cells, cells.shape[dim] - width, cells.shape[dim], axis=dim)
        cells = jnp.concatenate(
            [
                lax.ppermute(tail, axis, [(i, (i + 1) % count) for i in range(ends)]),
                cells,
                lax.ppermute(head, axis, [((i + 1) % count, i) for i in range(ends)]),
            ],
            axis=dim,
        )
    return cells


def difference_pair(padded, sweep_direction, length):
    shifted = [
        lax.slice_in_dim(padded, offset, offset + length, axis=sweep_direction)
        for offset in range(5)
    ]
    gradient = (8.0 * (shifted[3] - shifted[1]) - (shifted[4] - shifted[0])) / 12.0
    curvature = (
        16.0 * (shifted[3] + shifted[1]) - (shifted[4] + shifted[0]) - 30.0 * shifted[2]
    ) / 12.0
    return (gradient, curvature)


def build_rhs(field, courant, y_padded, x_padded):
    z_padded = jnp.concatenate([field[:, :, -2:], field, field[:, :, :2]], 2)
    grad_y, curve_y = difference_pair(y_padded, 0, field.shape[0])
    grad_x = difference_pair(x_padded, 1, field.shape[1])[0]
    grad_z, curve_z = difference_pair(z_padded, 2, field.shape[2])
    transport = courant[0] * grad_x + courant[1] * grad_y + courant[2] * grad_z
    return field - transport + 0.05 * (curve_y + curve_z) + 0.3 * field / (1.0 + field * field)


def rows_below(values, stride, fill, sweep_direction):
    length = values.shape[sweep_direction]
    filler = jnp.full_like(lax.slice_in_dim(values, 0, stride, axis=sweep_direction), fill)
    return jnp.concatenate(
        [filler, lax.slice_in_dim(values, 0, length - stride, axis=sweep_direction)],
        sweep_direction,
    )


def rows_above(values, stride, fill, sweep_direction):
    length = values.shape[sweep_direction]
    filler = jnp.full_like(
        lax.slice_in_dim(values, length - stride, length, axis=sweep_direction), fill
    )
    return jnp.concatenate(
        [lax.slice_in_dim(values, stride, length, axis=sweep_direction), filler], sweep_direction
    )


def combine_rows(own_rows, below_set, above_set):
    lower_band, main_diagonal, upper_band, right_hand_sides = own_rows
    low_sub, low_diag, low_super, low_rights = below_set
    high_sub, high_diag, high_super, high_rights = above_set
    factor_low = -lower_band / low_diag
    factor_high = -upper_band / high_diag
    new_sub = factor_low * low_sub
    new_super = factor_high * high_super
    new_diag = main_diagonal + factor_low * low_super + factor_high * high_sub
    new_rights = tuple(
        (
            value + factor_low * lower_value + factor_high * upper_value
            for value, lower_value, upper_value in zip(right_hand_sides, low_rights, high_rights)
        )
    )
    return (new_sub, new_diag, new_super, new_rights)


def parallel_cyclic_reduction(
    lower_band, main_diagonal, upper_band, right_hand_sides, sweep_direction
):
    length = main_diagonal.shape[sweep_direction]
    stride = 1
    while stride < length:
        below_set = (
            rows_below(lower_band, stride, 0.0, sweep_direction),
            rows_below(main_diagonal, stride, 1.0, sweep_direction),
            rows_below(upper_band, stride, 0.0, sweep_direction),
            tuple((rows_below(value, stride, 0.0, sweep_direction) for value in right_hand_sides)),
        )
        above_set = (
            rows_above(lower_band, stride, 0.0, sweep_direction),
            rows_above(main_diagonal, stride, 1.0, sweep_direction),
            rows_above(upper_band, stride, 0.0, sweep_direction),
            tuple((rows_above(value, stride, 0.0, sweep_direction) for value in right_hand_sides)),
        )
        lower_band, main_diagonal, upper_band, right_hand_sides = combine_rows(
            (lower_band, main_diagonal, upper_band, right_hand_sides), below_set, above_set
        )
        stride = stride * 2
    return tuple((value / main_diagonal for value in right_hand_sides))


def factor_kernel(rate_ref, ratio_ref, inverse_ref, first_ref, last_ref, lead_ref):
    rows = ratio_ref.shape[0]
    sublanes = ratio_ref.shape[1]

    def at(i):
        return pl.ds(i, sublanes, stride=rows)

    zero = jnp.zeros(ratio_ref.shape[1:], jnp.float32)
    rate = rate_ref[at(1)]
    inverse = 1.0 / (1.0 + 2.0 * rate)
    ratio = -rate * inverse
    first = rate * inverse
    ratio_ref[1] = ratio
    inverse_ref[1] = inverse
    lead_ref[1] = first

    def forward(i, carry):
        ratio, first, _ = carry
        rate = rate_ref[at(i)]
        inverse = 1.0 / ((1.0 + 2.0 * rate) + rate * ratio)
        ratio = -rate * inverse
        first = rate * first * inverse
        ratio_ref[i] = ratio
        inverse_ref[i] = inverse
        lead_ref[i] = first
        return ratio, first, inverse

    _, first, inverse = lax.fori_loop(2, rows - 1, forward, (ratio, first, zero), unroll=8)
    last = rate_ref[at(rows - 2)] * inverse
    first_ref[at(rows - 2)] = first
    last_ref[at(rows - 2)] = last

    def backward(j, carry):
        first, last = carry
        i = rows - 3 - j
        ratio = ratio_ref[i]
        first = lead_ref[i] - ratio * first
        last = -ratio * last
        first_ref[at(i)] = first
        last_ref[at(i)] = last
        return first, last

    lax.fori_loop(0, rows - 3, backward, (first, last), unroll=8)
    for ref in (first_ref, last_ref):
        ref[at(0)] = zero
        ref[at(rows - 1)] = zero


def substitute_kernel(rate_ref, right_ref, ratio_ref, inverse_ref, part_ref, ahead_ref):
    rows = ratio_ref.shape[0]
    sublanes = ratio_ref.shape[1]

    def at(i):
        return pl.ds(i, sublanes, stride=rows)

    zero = jnp.zeros(ratio_ref.shape[1:], jnp.float32)
    part = right_ref[at(1)] * inverse_ref[1]
    ahead_ref[1] = part

    def forward(i, part):
        part = (right_ref[at(i)] + rate_ref[at(i)] * part) * inverse_ref[i]
        ahead_ref[i] = part
        return part

    part = lax.fori_loop(2, rows - 1, forward, part, unroll=8)
    part_ref[at(rows - 2)] = part

    def backward(j, part):
        i = rows - 3 - j
        part = ahead_ref[i] - ratio_ref[i] * part
        part_ref[at(i)] = part
        return part

    lax.fori_loop(0, rows - 3, backward, part, unroll=8)
    part_ref[at(0)] = zero
    part_ref[at(rows - 1)] = zero


def local_factor(rate, chunks):
    planes, length, lanes = rate.shape
    rows = length // chunks
    flat = jax.ShapeDtypeStruct((planes * length, lanes), jnp.float32)
    table = jax.ShapeDtypeStruct((rows, planes * chunks, lanes), jnp.float32)
    return pl.pallas_call(
        factor_kernel,
        out_shape=(table, table, flat, flat),
        scratch_shapes=[pltpu.VMEM(table.shape, jnp.float32)],
    )(rate.reshape(planes * length, lanes))


def local_substitute(rate, right, ratio, inverse):
    planes, length, lanes = rate.shape
    flat = jax.ShapeDtypeStruct((planes * length, lanes), jnp.float32)
    return pl.pallas_call(
        substitute_kernel,
        out_shape=flat,
        scratch_shapes=[pltpu.VMEM(ratio.shape, jnp.float32)],
    )(rate.reshape(planes * length, lanes), right.reshape(planes * length, lanes), ratio, inverse)


def shards(field, courant, diffusion_number):
    chunks = 2
    y_padded = padded_2(field, (("gy", 0),), 2, True)
    x_padded = padded_2(field, (("gx", 1),), 2, False)
    rhs = build_rhs(field, courant, y_padded, x_padded)
    place = lax.axis_index("gx")
    device_count = lax.axis_size("gx")
    planes = field.shape[0]
    ratio, inverse, first, last = local_factor(diffusion_number, chunks)
    part = local_substitute(diffusion_number, rhs, ratio, inverse)
    rows = ratio.shape[0]
    part, first, last = (value.reshape(planes, chunks, rows, -1) for value in (part, first, last))
    rate = diffusion_number.reshape(planes, chunks, rows, -1)
    right = rhs.reshape(planes, chunks, rows, -1)
    low_open = (place > 0).astype(jnp.float32)
    high_open = (place < device_count - 1).astype(jnp.float32)
    chunk_of = lax.broadcasted_iota(jnp.int32, (1, chunks, 1), 1)
    low_scale = jnp.where(chunk_of == 0, low_open, 1.0)
    high_scale = jnp.where(chunk_of == chunks - 1, high_open, 1.0)
    rate_first, rate_last = rate[:, :, 0], rate[:, :, rows - 1]
    sub_first = -rate_first * low_scale
    diag_first = (1.0 + 2.0 * rate_first) - rate_first * first[:, :, 1]
    super_first = -rate_first * last[:, :, 1]
    right_first = right[:, :, 0] + rate_first * part[:, :, 1]
    sub_last = -rate_last * first[:, :, rows - 2]
    diag_last = (1.0 + 2.0 * rate_last) - rate_last * last[:, :, rows - 2]
    super_last = -rate_last * high_scale
    right_last = right[:, :, rows - 1] + rate_last * part[:, :, rows - 2]
    stacked = jnp.stack(
        [sub_first, sub_last, diag_first, diag_last, super_first, super_last, right_first, right_last], 2
    )
    lanes = stacked.shape[-1]
    stacked = stacked.reshape(planes, chunks * 8, lanes)
    gathered = lax.all_gather(stacked, "gx", axis=1, tiled=True)
    gathered = gathered.reshape(planes, device_count, chunks, 4, 2, lanes)
    gathered_lower_band, gathered_diagonal, gathered_upper_band, gathered_rhs = (
        gathered[:, :, :, k].reshape(planes, 2 * chunks * device_count, lanes) for k in range(4)
    )
    boundary_rows_gathered = parallel_cyclic_reduction(
        gathered_lower_band, gathered_diagonal, gathered_upper_band, (gathered_rhs,), 1
    )[0]
    ends = lax.dynamic_slice_in_dim(boundary_rows_gathered, 2 * chunks * place, 2 * chunks, 1)
    ends = ends.reshape(planes, chunks, 2, 1, lanes)
    start_value, end_value = ends[:, :, 0], ends[:, :, 1]
    solved = part + first * start_value + last * end_value
    row = lax.broadcasted_iota(jnp.int32, (1, 1, rows, 1), 2)
    solved = jnp.where(row == 0, start_value, solved)
    solved = jnp.where(row == rows - 1, end_value, solved)
    return solved.reshape(planes, chunks * rows, lanes)


def solution(mesh):
    in_specs = (P("gy", "gx", None), P(None, "gy", "gx", None), P("gy", "gx", None))
    out_specs = P("gy", "gx", None)
    return jax.shard_map(shards, mesh=mesh, in_specs=in_specs, out_specs=out_specs, check_vma=False)
```

```python
import jax
import jax.numpy as jnp
from jax import lax
from jax.sharding import PartitionSpec as P
from jax.experimental import pallas as pl
from jax.experimental.pallas import tpu as pltpu


def padded_2(cells, sides, width, closed):
    for axis, dim in sides:
        count = lax.axis_size(axis)
        ends = count if closed else count - 1
        head = lax.slice_in_dim(cells, 0, width, axis=dim)
        tail = lax.slice_in_dim(cells, cells.shape[dim] - width, cells.shape[dim], axis=dim)
        cells = jnp.concatenate(
            [
                lax.ppermute(tail, axis, [(i, (i + 1) % count) for i in range(ends)]),
                cells,
                lax.ppermute(head, axis, [((i + 1) % count, i) for i in range(ends)]),
            ],
            axis=dim,
        )
    return cells


def difference_pair(padded, sweep_direction, length):
    shifted = [
        lax.slice_in_dim(padded, offset, offset + length, axis=sweep_direction)
        for offset in range(5)
    ]
    gradient = (8.0 * (shifted[3] - shifted[1]) - (shifted[4] - shifted[0])) / 12.0
    curvature = (
        16.0 * (shifted[3] + shifted[1]) - (shifted[4] + shifted[0]) - 30.0 * shifted[2]
    ) / 12.0
    return (gradient, curvature)


def build_rhs(field, courant, y_padded, x_padded):
    z_padded = jnp.concatenate([field[:, :, -2:], field, field[:, :, :2]], 2)
    grad_y, curve_y = difference_pair(y_padded, 0, field.shape[0])
    grad_x = difference_pair(x_padded, 1, field.shape[1])[0]
    grad_z, curve_z = difference_pair(z_padded, 2, field.shape[2])
    transport = courant[0] * grad_x + courant[1] * grad_y + courant[2] * grad_z
    return field - transport + 0.05 * (curve_y + curve_z) + 0.3 * field / (1.0 + field * field)


def rows_below(values, stride, fill, sweep_direction):
    length = values.shape[sweep_direction]
    filler = jnp.full_like(lax.slice_in_dim(values, 0, stride, axis=sweep_direction), fill)
    return jnp.concatenate(
        [filler, lax.slice_in_dim(values, 0, length - stride, axis=sweep_direction)],
        sweep_direction,
    )


def rows_above(values, stride, fill, sweep_direction):
    length = values.shape[sweep_direction]
    filler = jnp.full_like(
        lax.slice_in_dim(values, length - stride, length, axis=sweep_direction), fill
    )
    return jnp.concatenate(
        [lax.slice_in_dim(values, stride, length, axis=sweep_direction), filler], sweep_direction
    )


def combine_rows(own_rows, below_set, above_set):
    lower_band, main_diagonal, upper_band, right_hand_sides = own_rows
    low_sub, low_diag, low_super, low_rights = below_set
    high_sub, high_diag, high_super, high_rights = above_set
    factor_low = -lower_band / low_diag
    factor_high = -upper_band / high_diag
    new_sub = factor_low * low_sub
    new_super = factor_high * high_super
    new_diag = main_diagonal + factor_low * low_super + factor_high * high_sub
    new_rights = tuple(
        (
            value + factor_low * lower_value + factor_high * upper_value
            for value, lower_value, upper_value in zip(right_hand_sides, low_rights, high_rights)
        )
    )
    return (new_sub, new_diag, new_super, new_rights)


def parallel_cyclic_reduction(
    lower_band, main_diagonal, upper_band, right_hand_sides, sweep_direction
):
    length = main_diagonal.shape[sweep_direction]
    stride = 1
    while stride < length:
        below_set = (
            rows_below(lower_band, stride, 0.0, sweep_direction),
            rows_below(main_diagonal, stride, 1.0, sweep_direction),
            rows_below(upper_band, stride, 0.0, sweep_direction),
            tuple((rows_below(value, stride, 0.0, sweep_direction) for value in right_hand_sides)),
        )
        above_set = (
            rows_above(lower_band, stride, 0.0, sweep_direction),
            rows_above(main_diagonal, stride, 1.0, sweep_direction),
            rows_above(upper_band, stride, 0.0, sweep_direction),
            tuple((rows_above(value, stride, 0.0, sweep_direction) for value in right_hand_sides)),
        )
        lower_band, main_diagonal, upper_band, right_hand_sides = combine_rows(
            (lower_band, main_diagonal, upper_band, right_hand_sides), below_set, above_set
        )
        stride = stride * 2
    return tuple((value / main_diagonal for value in right_hand_sides))


def thomas_kernel(rate_ref, right_ref, part_ref, first_ref, last_ref, ratio_ref, ahead_ref, lead_ref):
    rows = ratio_ref.shape[0]
    sublanes = ratio_ref.shape[1]

    def at(i):
        return pl.ds(i, sublanes, stride=rows)

    zero = jnp.zeros(ratio_ref.shape[1:], jnp.float32)
    rate = rate_ref[at(1)]
    inverse = 1.0 / (1.0 + 2.0 * rate)
    ratio = -rate * inverse
    part = right_ref[at(1)] * inverse
    first = rate * inverse
    ratio_ref[1] = ratio
    ahead_ref[1] = part
    lead_ref[1] = first

    def forward(i, carry):
        ratio, part, first, _ = carry
        rate = rate_ref[at(i)]
        inverse = 1.0 / ((1.0 + 2.0 * rate) + rate * ratio)
        ratio = -rate * inverse
        part = (right_ref[at(i)] + rate * part) * inverse
        first = rate * first * inverse
        ratio_ref[i] = ratio
        ahead_ref[i] = part
        lead_ref[i] = first
        return ratio, part, first, inverse

    _, part, first, inverse = lax.fori_loop(
        2, rows - 1, forward, (ratio, part, first, zero), unroll=8
    )
    last = rate_ref[at(rows - 2)] * inverse
    part_ref[at(rows - 2)] = part
    first_ref[at(rows - 2)] = first
    last_ref[at(rows - 2)] = last

    def backward(j, carry):
        part, first, last = carry
        i = rows - 3 - j
        ratio = ratio_ref[i]
        part = ahead_ref[i] - ratio * part
        first = lead_ref[i] - ratio * first
        last = -ratio * last
        part_ref[at(i)] = part
        first_ref[at(i)] = first
        last_ref[at(i)] = last
        return part, first, last

    lax.fori_loop(0, rows - 3, backward, (part, first, last), unroll=8)
    for ref in (part_ref, first_ref, last_ref):
        ref[at(0)] = zero
        ref[at(rows - 1)] = zero


def local_solve(rate, right, chunks):
    planes, length, lanes = rate.shape
    rows = length // chunks
    flat = jax.ShapeDtypeStruct((planes * length, lanes), jnp.float32)
    scratch = pltpu.VMEM((rows, planes * chunks, lanes), jnp.float32)
    outs = pl.pallas_call(
        thomas_kernel,
        out_shape=(flat, flat, flat),
        scratch_shapes=[scratch, scratch, scratch],
    )(rate.reshape(planes * length, lanes), right.reshape(planes * length, lanes))
    return tuple(out.reshape(planes, chunks, rows, lanes) for out in outs)


def shards(field, courant, diffusion_number):
    chunks = 2
    y_padded = padded_2(field, (("gy", 0),), 2, True)
    x_padded = padded_2(field, (("gx", 1),), 2, False)
    flat = jnp.zeros_like(field[:2])
    own_rhs = build_rhs(field, courant, jnp.concatenate([flat, field, flat], 0), x_padded)
    own_rhs = lax.optimization_barrier(own_rhs)
    halo_only = jnp.concatenate([y_padded[:2], jnp.zeros_like(field), y_padded[-2:]], 0)
    grad_y, curve_y = difference_pair(halo_only, 0, field.shape[0])
    rhs = own_rhs + (0.05 * curve_y - courant[1] * grad_y)
    place = lax.axis_index("gx")
    device_count = lax.axis_size("gx")
    planes = field.shape[0]
    part, first, last = local_solve(diffusion_number, rhs, chunks)
    rows = part.shape[2]
    rate = diffusion_number.reshape(planes, chunks, rows, -1)
    right = rhs.reshape(planes, chunks, rows, -1)
    low_open = (place > 0).astype(jnp.float32)
    high_open = (place < device_count - 1).astype(jnp.float32)
    chunk_of = lax.broadcasted_iota(jnp.int32, (1, chunks, 1), 1)
    low_scale = jnp.where(chunk_of == 0, low_open, 1.0)
    high_scale = jnp.where(chunk_of == chunks - 1, high_open, 1.0)
    rate_first, rate_last = rate[:, :, 0], rate[:, :, rows - 1]
    sub_first = -rate_first * low_scale
    diag_first = (1.0 + 2.0 * rate_first) - rate_first * first[:, :, 1]
    super_first = -rate_first * last[:, :, 1]
    right_first = right[:, :, 0] + rate_first * part[:, :, 1]
    sub_last = -rate_last * first[:, :, rows - 2]
    diag_last = (1.0 + 2.0 * rate_last) - rate_last * last[:, :, rows - 2]
    super_last = -rate_last * high_scale
    right_last = right[:, :, rows - 1] + rate_last * part[:, :, rows - 2]
    stacked = jnp.stack(
        [sub_first, sub_last, diag_first, diag_last, super_first, super_last, right_first, right_last], 2
    )
    lanes = stacked.shape[-1]
    stacked = stacked.reshape(planes, chunks * 8, lanes)
    gathered = lax.all_gather(stacked, "gx", axis=1, tiled=True)
    gathered = gathered.reshape(planes, device_count, chunks, 4, 2, lanes)
    gathered_lower_band, gathered_diagonal, gathered_upper_band, gathered_rhs = (
        gathered[:, :, :, k].reshape(planes, 2 * chunks * device_count, lanes) for k in range(4)
    )
    boundary_rows_gathered = parallel_cyclic_reduction(
        gathered_lower_band, gathered_diagonal, gathered_upper_band, (gathered_rhs,), 1
    )[0]
    ends = lax.dynamic_slice_in_dim(boundary_rows_gathered, 2 * chunks * place, 2 * chunks, 1)
    ends = ends.reshape(planes, chunks, 2, 1, lanes)
    start_value, end_value = ends[:, :, 0], ends[:, :, 1]
    solved = part + first * start_value + last * end_value
    row = lax.broadcasted_iota(jnp.int32, (1, 1, rows, 1), 2)
    solved = jnp.where(row == 0, start_value, solved)
    solved = jnp.where(row == rows - 1, end_value, solved)
    return solved.reshape(planes, chunks * rows, lanes)


def solution(mesh):
    in_specs = (P("gy", "gx", None), P(None, "gy", "gx", None), P("gy", "gx", None))
    out_specs = P("gy", "gx", None)
    return jax.shard_map(shards, mesh=mesh, in_specs=in_specs, out_specs=out_specs, check_vma=False)
```

```python
import jax
import jax.numpy as jnp
from jax import lax
from jax.sharding import PartitionSpec as P
from jax.experimental import pallas as pl
from jax.experimental.pallas import tpu as pltpu


def padded_2(cells, sides, width, closed):
    for axis, dim in sides:
        count = lax.axis_size(axis)
        ends = count if closed else count - 1
        head = lax.slice_in_dim(cells, 0, width, axis=dim)
        tail = lax.slice_in_dim(cells, cells.shape[dim] - width, cells.shape[dim], axis=dim)
        cells = jnp.concatenate(
            [
                lax.ppermute(tail, axis, [(i, (i + 1) % count) for i in range(ends)]),
                cells,
                lax.ppermute(head, axis, [((i + 1) % count, i) for i in range(ends)]),
            ],
            axis=dim,
        )
    return cells


def difference_pair(padded, sweep_direction, length):
    shifted = [
        lax.slice_in_dim(padded, offset, offset + length, axis=sweep_direction)
        for offset in range(5)
    ]
    gradient = (8.0 * (shifted[3] - shifted[1]) - (shifted[4] - shifted[0])) / 12.0
    curvature = (
        16.0 * (shifted[3] + shifted[1]) - (shifted[4] + shifted[0]) - 30.0 * shifted[2]
    ) / 12.0
    return (gradient, curvature)


def build_rhs(field, courant, y_padded, x_padded):
    z_padded = jnp.concatenate([field[:, :, -2:], field, field[:, :, :2]], 2)
    grad_y, curve_y = difference_pair(y_padded, 0, field.shape[0])
    grad_x = difference_pair(x_padded, 1, field.shape[1])[0]
    grad_z, curve_z = difference_pair(z_padded, 2, field.shape[2])
    transport = courant[0] * grad_x + courant[1] * grad_y + courant[2] * grad_z
    return field - transport + 0.05 * (curve_y + curve_z) + 0.3 * field / (1.0 + field * field)


def rows_below(values, stride, fill, sweep_direction):
    length = values.shape[sweep_direction]
    filler = jnp.full_like(lax.slice_in_dim(values, 0, stride, axis=sweep_direction), fill)
    return jnp.concatenate(
        [filler, lax.slice_in_dim(values, 0, length - stride, axis=sweep_direction)],
        sweep_direction,
    )


def rows_above(values, stride, fill, sweep_direction):
    length = values.shape[sweep_direction]
    filler = jnp.full_like(
        lax.slice_in_dim(values, length - stride, length, axis=sweep_direction), fill
    )
    return jnp.concatenate(
        [lax.slice_in_dim(values, stride, length, axis=sweep_direction), filler], sweep_direction
    )


def combine_rows(own_rows, below_set, above_set):
    lower_band, main_diagonal, upper_band, right_hand_sides = own_rows
    low_sub, low_diag, low_super, low_rights = below_set
    high_sub, high_diag, high_super, high_rights = above_set
    factor_low = -lower_band / low_diag
    factor_high = -upper_band / high_diag
    new_sub = factor_low * low_sub
    new_super = factor_high * high_super
    new_diag = main_diagonal + factor_low * low_super + factor_high * high_sub
    new_rights = tuple(
        (
            value + factor_low * lower_value + factor_high * upper_value
            for value, lower_value, upper_value in zip(right_hand_sides, low_rights, high_rights)
        )
    )
    return (new_sub, new_diag, new_super, new_rights)


def parallel_cyclic_reduction(
    lower_band, main_diagonal, upper_band, right_hand_sides, sweep_direction
):
    length = main_diagonal.shape[sweep_direction]
    stride = 1
    while stride < length:
        below_set = (
            rows_below(lower_band, stride, 0.0, sweep_direction),
            rows_below(main_diagonal, stride, 1.0, sweep_direction),
            rows_below(upper_band, stride, 0.0, sweep_direction),
            tuple((rows_below(value, stride, 0.0, sweep_direction) for value in right_hand_sides)),
        )
        above_set = (
            rows_above(lower_band, stride, 0.0, sweep_direction),
            rows_above(main_diagonal, stride, 1.0, sweep_direction),
            rows_above(upper_band, stride, 0.0, sweep_direction),
            tuple((rows_above(value, stride, 0.0, sweep_direction) for value in right_hand_sides)),
        )
        lower_band, main_diagonal, upper_band, right_hand_sides = combine_rows(
            (lower_band, main_diagonal, upper_band, right_hand_sides), below_set, above_set
        )
        stride = stride * 2
    return tuple((value / main_diagonal for value in right_hand_sides))


def thomas_kernel(rate_ref, right_ref, part_ref, first_ref, last_ref, ratio_ref, ahead_ref, lead_ref):
    rows = ratio_ref.shape[0]
    sublanes = ratio_ref.shape[1]

    def at(i):
        return pl.ds(i, sublanes, stride=rows)

    zero = jnp.zeros(ratio_ref.shape[1:], jnp.float32)
    rate = rate_ref[at(1)]
    inverse = 1.0 / (1.0 + 2.0 * rate)
    ratio = -rate * inverse
    part = right_ref[at(1)] * inverse
    first = rate * inverse
    ratio_ref[1] = ratio
    ahead_ref[1] = part
    lead_ref[1] = first

    def forward(i, carry):
        ratio, part, first, _ = carry
        rate = rate_ref[at(i)]
        inverse = 1.0 / ((1.0 + 2.0 * rate) + rate * ratio)
        ratio = -rate * inverse
        part = (right_ref[at(i)] + rate * part) * inverse
        first = rate * first * inverse
        ratio_ref[i] = ratio
        ahead_ref[i] = part
        lead_ref[i] = first
        return ratio, part, first, inverse

    _, part, first, inverse = lax.fori_loop(
        2, rows - 1, forward, (ratio, part, first, zero), unroll=True
    )
    last = rate_ref[at(rows - 2)] * inverse
    part_ref[at(rows - 2)] = part
    first_ref[at(rows - 2)] = first
    last_ref[at(rows - 2)] = last

    def backward(j, carry):
        part, first, last = carry
        i = rows - 3 - j
        ratio = ratio_ref[i]
        part = ahead_ref[i] - ratio * part
        first = lead_ref[i] - ratio * first
        last = -ratio * last
        part_ref[at(i)] = part
        first_ref[at(i)] = first
        last_ref[at(i)] = last
        return part, first, last

    lax.fori_loop(0, rows - 3, backward, (part, first, last), unroll=True)
    for ref in (part_ref, first_ref, last_ref):
        ref[at(0)] = zero
        ref[at(rows - 1)] = zero


def local_solve(rate, right, chunks):
    planes, length, lanes = rate.shape
    rows = length // chunks
    flat = jax.ShapeDtypeStruct((planes * length, lanes), jnp.float32)
    scratch = pltpu.VMEM((rows, planes * chunks, lanes), jnp.float32)
    outs = pl.pallas_call(
        thomas_kernel,
        out_shape=(flat, flat, flat),
        scratch_shapes=[scratch, scratch, scratch],
    )(rate.reshape(planes * length, lanes), right.reshape(planes * length, lanes))
    return tuple(out.reshape(planes, chunks, rows, lanes) for out in outs)


def shards(field, courant, diffusion_number):
    chunks = 2
    y_padded = padded_2(field, (("gy", 0),), 2, True)
    x_padded = padded_2(field, (("gx", 1),), 2, False)
    rhs = build_rhs(field, courant, y_padded, x_padded)
    place = lax.axis_index("gx")
    device_count = lax.axis_size("gx")
    planes = field.shape[0]
    part, first, last = local_solve(diffusion_number, rhs, chunks)
    rows = part.shape[2]
    rate = diffusion_number.reshape(planes, chunks, rows, -1)
    right = rhs.reshape(planes, chunks, rows, -1)
    low_open = (place > 0).astype(jnp.float32)
    high_open = (place < device_count - 1).astype(jnp.float32)
    chunk_of = lax.broadcasted_iota(jnp.int32, (1, chunks, 1), 1)
    low_scale = jnp.where(chunk_of == 0, low_open, 1.0)
    high_scale = jnp.where(chunk_of == chunks - 1, high_open, 1.0)
    rate_first, rate_last = rate[:, :, 0], rate[:, :, rows - 1]
    sub_first = -rate_first * low_scale
    diag_first = (1.0 + 2.0 * rate_first) - rate_first * first[:, :, 1]
    super_first = -rate_first * last[:, :, 1]
    right_first = right[:, :, 0] + rate_first * part[:, :, 1]
    sub_last = -rate_last * first[:, :, rows - 2]
    diag_last = (1.0 + 2.0 * rate_last) - rate_last * last[:, :, rows - 2]
    super_last = -rate_last * high_scale
    right_last = right[:, :, rows - 1] + rate_last * part[:, :, rows - 2]
    stacked = jnp.stack(
        [sub_first, sub_last, diag_first, diag_last, super_first, super_last, right_first, right_last], 2
    )
    lanes = stacked.shape[-1]
    stacked = stacked.reshape(planes, chunks * 8, lanes)
    gathered = lax.all_gather(stacked, "gx", axis=1, tiled=True)
    gathered = gathered.reshape(planes, device_count, chunks, 4, 2, lanes)
    gathered_lower_band, gathered_diagonal, gathered_upper_band, gathered_rhs = (
        gathered[:, :, :, k].reshape(planes, 2 * chunks * device_count, lanes) for k in range(4)
    )
    boundary_rows_gathered = parallel_cyclic_reduction(
        gathered_lower_band, gathered_diagonal, gathered_upper_band, (gathered_rhs,), 1
    )[0]
    ends = lax.dynamic_slice_in_dim(boundary_rows_gathered, 2 * chunks * place, 2 * chunks, 1)
    ends = ends.reshape(planes, chunks, 2, 1, lanes)
    start_value, end_value = ends[:, :, 0], ends[:, :, 1]
    solved = part + first * start_value + last * end_value
    row = lax.broadcasted_iota(jnp.int32, (1, 1, rows, 1), 2)
    solved = jnp.where(row == 0, start_value, solved)
    solved = jnp.where(row == rows - 1, end_value, solved)
    return solved.reshape(planes, chunks * rows, lanes)


def solution(mesh):
    in_specs = (P("gy", "gx", None), P(None, "gy", "gx", None), P("gy", "gx", None))
    out_specs = P("gy", "gx", None)
    return jax.shard_map(shards, mesh=mesh, in_specs=in_specs, out_specs=out_specs, check_vma=False)
```

```python
import functools

import jax
import jax.numpy as jnp
from jax import lax
from jax.sharding import PartitionSpec as P
from jax.experimental import pallas as pl
from jax.experimental.pallas import tpu as pltpu


def padded_2(cells, sides, width, closed):
    for axis, dim in sides:
        count = lax.axis_size(axis)
        ends = count if closed else count - 1
        head = lax.slice_in_dim(cells, 0, width, axis=dim)
        tail = lax.slice_in_dim(cells, cells.shape[dim] - width, cells.shape[dim], axis=dim)
        cells = jnp.concatenate(
            [
                lax.ppermute(tail, axis, [(i, (i + 1) % count) for i in range(ends)]),
                cells,
                lax.ppermute(head, axis, [((i + 1) % count, i) for i in range(ends)]),
            ],
            axis=dim,
        )
    return cells


def difference_pair(padded, sweep_direction, length):
    shifted = [
        lax.slice_in_dim(padded, offset, offset + length, axis=sweep_direction)
        for offset in range(5)
    ]
    gradient = (8.0 * (shifted[3] - shifted[1]) - (shifted[4] - shifted[0])) / 12.0
    curvature = (
        16.0 * (shifted[3] + shifted[1]) - (shifted[4] + shifted[0]) - 30.0 * shifted[2]
    ) / 12.0
    return (gradient, curvature)


def build_rhs(field, courant, y_padded, x_padded):
    z_padded = jnp.concatenate([field[:, :, -2:], field, field[:, :, :2]], 2)
    grad_y, curve_y = difference_pair(y_padded, 0, field.shape[0])
    grad_x = difference_pair(x_padded, 1, field.shape[1])[0]
    grad_z, curve_z = difference_pair(z_padded, 2, field.shape[2])
    transport = courant[0] * grad_x + courant[1] * grad_y + courant[2] * grad_z
    return field - transport + 0.05 * (curve_y + curve_z) + 0.3 * field / (1.0 + field * field)


def rows_below(values, stride, fill, sweep_direction):
    length = values.shape[sweep_direction]
    filler = jnp.full_like(lax.slice_in_dim(values, 0, stride, axis=sweep_direction), fill)
    return jnp.concatenate(
        [filler, lax.slice_in_dim(values, 0, length - stride, axis=sweep_direction)],
        sweep_direction,
    )


def rows_above(values, stride, fill, sweep_direction):
    length = values.shape[sweep_direction]
    filler = jnp.full_like(
        lax.slice_in_dim(values, length - stride, length, axis=sweep_direction), fill
    )
    return jnp.concatenate(
        [lax.slice_in_dim(values, stride, length, axis=sweep_direction), filler], sweep_direction
    )


def combine_rows(own_rows, below_set, above_set):
    lower_band, main_diagonal, upper_band, right_hand_sides = own_rows
    low_sub, low_diag, low_super, low_rights = below_set
    high_sub, high_diag, high_super, high_rights = above_set
    factor_low = -lower_band / low_diag
    factor_high = -upper_band / high_diag
    new_sub = factor_low * low_sub
    new_super = factor_high * high_super
    new_diag = main_diagonal + factor_low * low_super + factor_high * high_sub
    new_rights = tuple(
        (
            value + factor_low * lower_value + factor_high * upper_value
            for value, lower_value, upper_value in zip(right_hand_sides, low_rights, high_rights)
        )
    )
    return (new_sub, new_diag, new_super, new_rights)


def parallel_cyclic_reduction(
    lower_band, main_diagonal, upper_band, right_hand_sides, sweep_direction
):
    length = main_diagonal.shape[sweep_direction]
    stride = 1
    while stride < length:
        below_set = (
            rows_below(lower_band, stride, 0.0, sweep_direction),
            rows_below(main_diagonal, stride, 1.0, sweep_direction),
            rows_below(upper_band, stride, 0.0, sweep_direction),
            tuple((rows_below(value, stride, 0.0, sweep_direction) for value in right_hand_sides)),
        )
        above_set = (
            rows_above(lower_band, stride, 0.0, sweep_direction),
            rows_above(main_diagonal, stride, 1.0, sweep_direction),
            rows_above(upper_band, stride, 0.0, sweep_direction),
            tuple((rows_above(value, stride, 0.0, sweep_direction) for value in right_hand_sides)),
        )
        lower_band, main_diagonal, upper_band, right_hand_sides = combine_rows(
            (lower_band, main_diagonal, upper_band, right_hand_sides), below_set, above_set
        )
        stride = stride * 2
    return tuple((value / main_diagonal for value in right_hand_sides))


def thomas_kernel(rate_ref, right_ref, part_ref, first_ref, last_ref, ratio_ref, ahead_ref, lead_ref):
    rows = ratio_ref.shape[0]
    sublanes = ratio_ref.shape[1]

    def at(i):
        return pl.ds(i, sublanes, stride=rows)

    zero = jnp.zeros(ratio_ref.shape[1:], jnp.float32)
    rate = rate_ref[at(1)]
    inverse = 1.0 / (1.0 + 2.0 * rate)
    ratio = -rate * inverse
    part = right_ref[at(1)] * inverse
    first = rate * inverse
    ratio_ref[1] = ratio
    ahead_ref[1] = part
    lead_ref[1] = first

    def forward(i, carry):
        ratio, part, first, _ = carry
        rate = rate_ref[at(i)]
        inverse = 1.0 / ((1.0 + 2.0 * rate) + rate * ratio)
        ratio = -rate * inverse
        part = (right_ref[at(i)] + rate * part) * inverse
        first = rate * first * inverse
        ratio_ref[i] = ratio
        ahead_ref[i] = part
        lead_ref[i] = first
        return ratio, part, first, inverse

    _, part, first, inverse = lax.fori_loop(
        2, rows - 1, forward, (ratio, part, first, zero), unroll=True
    )
    last = rate_ref[at(rows - 2)] * inverse
    part_ref[at(rows - 2)] = part
    first_ref[at(rows - 2)] = first
    last_ref[at(rows - 2)] = last

    def backward(j, carry):
        part, first, last = carry
        i = rows - 3 - j
        ratio = ratio_ref[i]
        part = ahead_ref[i] - ratio * part
        first = lead_ref[i] - ratio * first
        last = -ratio * last
        part_ref[at(i)] = part
        first_ref[at(i)] = first
        last_ref[at(i)] = last
        return part, first, last

    lax.fori_loop(0, rows - 3, backward, (part, first, last), unroll=True)
    for ref in (part_ref, first_ref, last_ref):
        ref[at(0)] = zero
        ref[at(rows - 1)] = zero


def local_solve(rate, right, chunks):
    planes, length, lanes = rate.shape
    rows = length // chunks
    flat = jax.ShapeDtypeStruct((planes * length, lanes), jnp.float32)
    scratch = pltpu.VMEM((rows, planes * chunks, lanes), jnp.float32)
    outs = pl.pallas_call(
        thomas_kernel,
        out_shape=(flat, flat, flat),
        scratch_shapes=[scratch, scratch, scratch],
    )(rate.reshape(planes * length, lanes), right.reshape(planes * length, lanes))
    return tuple(out.reshape(planes, chunks, rows, lanes) for out in outs)


def finish_kernel(chunks, place_ref, system_ref, part_ref, first_ref, last_ref, out_ref, ratio_ref, value_ref):
    count, planes, lanes = ratio_ref.shape
    width = system_ref.shape[0] // planes
    length = part_ref.shape[0] // planes
    rows = length // chunks

    def coefficient(row, kind):
        return system_ref[pl.ds((row // 2) * 8 + kind * 2 + row % 2, planes, stride=width)]

    ratio = value = None
    for row in range(count):
        sub, diag, upper, right = (coefficient(row, kind) for kind in range(4))
        if row == 0:
            inverse = 1.0 / diag
            value = right * inverse
        else:
            inverse = 1.0 / (diag - sub * ratio)
            value = (right - sub * value) * inverse
        ratio = upper * inverse
        ratio_ref[row] = ratio
        value_ref[row] = value
    for row in range(count - 2, -1, -1):
        value = value_ref[row] - ratio_ref[row] * value
        value_ref[row] = value
    own = place_ref[0] * (2 * chunks)
    for chunk in range(chunks):
        for plane in range(planes):
            start_value = value_ref[own + 2 * chunk, pl.ds(plane, 1), :]
            end_value = value_ref[own + 2 * chunk + 1, pl.ds(plane, 1), :]
            offset = plane * length + chunk * rows
            block = pl.ds(offset, rows)
            out_ref[block] = part_ref[block] + first_ref[block] * start_value + last_ref[block] * end_value
            out_ref[pl.ds(offset, 1)] = start_value
            out_ref[pl.ds(offset + rows - 1, 1)] = end_value


def finish(place, system, part, first, last, chunks):
    planes, width, lanes = system.shape
    count = width // 8 * 2
    table = pltpu.VMEM((count, planes, lanes), jnp.float32)
    return pl.pallas_call(
        functools.partial(finish_kernel, chunks),
        out_shape=jax.ShapeDtypeStruct(part.shape, jnp.float32),
        in_specs=[pl.BlockSpec(memory_space=pltpu.SMEM)]
        + [pl.BlockSpec(memory_space=pltpu.VMEM)] * 4,
        out_specs=pl.BlockSpec(memory_space=pltpu.VMEM),
        scratch_shapes=[table, table],
    )(place.reshape(1).astype(jnp.int32), system.reshape(planes * width, lanes), part, first, last)


def shards(field, courant, diffusion_number):
    chunks = 2
    y_padded = padded_2(field, (("gy", 0),), 2, True)
    x_padded = padded_2(field, (("gx", 1),), 2, False)
    rhs = build_rhs(field, courant, y_padded, x_padded)
    place = lax.axis_index("gx")
    device_count = lax.axis_size("gx")
    planes = field.shape[0]
    part, first, last = local_solve(diffusion_number, rhs, chunks)
    rows = part.shape[2]
    rate = diffusion_number.reshape(planes, chunks, rows, -1)
    right = rhs.reshape(planes, chunks, rows, -1)
    low_open = (place > 0).astype(jnp.float32)
    high_open = (place < device_count - 1).astype(jnp.float32)
    chunk_of = lax.broadcasted_iota(jnp.int32, (1, chunks, 1), 1)
    low_scale = jnp.where(chunk_of == 0, low_open, 1.0)
    high_scale = jnp.where(chunk_of == chunks - 1, high_open, 1.0)
    rate_first, rate_last = rate[:, :, 0], rate[:, :, rows - 1]
    sub_first = -rate_first * low_scale
    diag_first = (1.0 + 2.0 * rate_first) - rate_first * first[:, :, 1]
    super_first = -rate_first * last[:, :, 1]
    right_first = right[:, :, 0] + rate_first * part[:, :, 1]
    sub_last = -rate_last * first[:, :, rows - 2]
    diag_last = (1.0 + 2.0 * rate_last) - rate_last * last[:, :, rows - 2]
    super_last = -rate_last * high_scale
    right_last = right[:, :, rows - 1] + rate_last * part[:, :, rows - 2]
    stacked = jnp.stack(
        [sub_first, sub_last, diag_first, diag_last, super_first, super_last, right_first, right_last], 2
    )
    lanes = stacked.shape[-1]
    stacked = stacked.reshape(planes, chunks * 8, lanes)
    gathered = lax.all_gather(stacked, "gx", axis=1, tiled=True)
    length = field.shape[1]
    flat = [value.reshape(planes * length, lanes) for value in (part, first, last)]
    solved = finish(place, gathered, *flat, chunks)
    return solved.reshape(planes, length, lanes)


def solution(mesh):
    in_specs = (P("gy", "gx", None), P(None, "gy", "gx", None), P("gy", "gx", None))
    out_specs = P("gy", "gx", None)
    return jax.shard_map(shards, mesh=mesh, in_specs=in_specs, out_specs=out_specs, check_vma=False)
```

```python
import functools

import jax
import jax.numpy as jnp
from jax import lax
from jax.sharding import PartitionSpec as P
from jax.experimental import pallas as pl
from jax.experimental.pallas import tpu as pltpu


def padded_2(cells, sides, width, closed):
    for axis, dim in sides:
        count = lax.axis_size(axis)
        ends = count if closed else count - 1
        head = lax.slice_in_dim(cells, 0, width, axis=dim)
        tail = lax.slice_in_dim(cells, cells.shape[dim] - width, cells.shape[dim], axis=dim)
        cells = jnp.concatenate(
            [
                lax.ppermute(tail, axis, [(i, (i + 1) % count) for i in range(ends)]),
                cells,
                lax.ppermute(head, axis, [((i + 1) % count, i) for i in range(ends)]),
            ],
            axis=dim,
        )
    return cells


def difference_pair(padded, sweep_direction, length):
    shifted = [
        lax.slice_in_dim(padded, offset, offset + length, axis=sweep_direction)
        for offset in range(5)
    ]
    gradient = (8.0 * (shifted[3] - shifted[1]) - (shifted[4] - shifted[0])) / 12.0
    curvature = (
        16.0 * (shifted[3] + shifted[1]) - (shifted[4] + shifted[0]) - 30.0 * shifted[2]
    ) / 12.0
    return (gradient, curvature)


def build_rhs(field, courant, y_padded, x_padded):
    z_padded = jnp.concatenate([field[:, :, -2:], field, field[:, :, :2]], 2)
    grad_y, curve_y = difference_pair(y_padded, 0, field.shape[0])
    grad_x = difference_pair(x_padded, 1, field.shape[1])[0]
    grad_z, curve_z = difference_pair(z_padded, 2, field.shape[2])
    transport = courant[0] * grad_x + courant[1] * grad_y + courant[2] * grad_z
    return field - transport + 0.05 * (curve_y + curve_z) + 0.3 * field / (1.0 + field * field)


def rows_below(values, stride, fill, sweep_direction):
    length = values.shape[sweep_direction]
    filler = jnp.full_like(lax.slice_in_dim(values, 0, stride, axis=sweep_direction), fill)
    return jnp.concatenate(
        [filler, lax.slice_in_dim(values, 0, length - stride, axis=sweep_direction)],
        sweep_direction,
    )


def rows_above(values, stride, fill, sweep_direction):
    length = values.shape[sweep_direction]
    filler = jnp.full_like(
        lax.slice_in_dim(values, length - stride, length, axis=sweep_direction), fill
    )
    return jnp.concatenate(
        [lax.slice_in_dim(values, stride, length, axis=sweep_direction), filler], sweep_direction
    )


def combine_rows(own_rows, below_set, above_set):
    lower_band, main_diagonal, upper_band, right_hand_sides = own_rows
    low_sub, low_diag, low_super, low_rights = below_set
    high_sub, high_diag, high_super, high_rights = above_set
    factor_low = -lower_band / low_diag
    factor_high = -upper_band / high_diag
    new_sub = factor_low * low_sub
    new_super = factor_high * high_super
    new_diag = main_diagonal + factor_low * low_super + factor_high * high_sub
    new_rights = tuple(
        (
            value + factor_low * lower_value + factor_high * upper_value
            for value, lower_value, upper_value in zip(right_hand_sides, low_rights, high_rights)
        )
    )
    return (new_sub, new_diag, new_super, new_rights)


def parallel_cyclic_reduction(
    lower_band, main_diagonal, upper_band, right_hand_sides, sweep_direction
):
    length = main_diagonal.shape[sweep_direction]
    stride = 1
    while stride < length:
        below_set = (
            rows_below(lower_band, stride, 0.0, sweep_direction),
            rows_below(main_diagonal, stride, 1.0, sweep_direction),
            rows_below(upper_band, stride, 0.0, sweep_direction),
            tuple((rows_below(value, stride, 0.0, sweep_direction) for value in right_hand_sides)),
        )
        above_set = (
            rows_above(lower_band, stride, 0.0, sweep_direction),
            rows_above(main_diagonal, stride, 1.0, sweep_direction),
            rows_above(upper_band, stride, 0.0, sweep_direction),
            tuple((rows_above(value, stride, 0.0, sweep_direction) for value in right_hand_sides)),
        )
        lower_band, main_diagonal, upper_band, right_hand_sides = combine_rows(
            (lower_band, main_diagonal, upper_band, right_hand_sides), below_set, above_set
        )
        stride = stride * 2
    return tuple((value / main_diagonal for value in right_hand_sides))


def thomas_kernel(
    chunks, devices, place_ref, rate_ref, right_ref,
    part_ref, first_ref, last_ref, system_ref, ratio_ref, ahead_ref, lead_ref,
):
    rows = ratio_ref.shape[0]
    sublanes = ratio_ref.shape[1]

    def at(i):
        return pl.ds(i, sublanes, stride=rows)

    zero = jnp.zeros(ratio_ref.shape[1:], jnp.float32)
    rate = rate_ref[at(1)]
    inverse = 1.0 / (1.0 + 2.0 * rate)
    ratio = -rate * inverse
    part = right_ref[at(1)] * inverse
    first = rate * inverse
    ratio_ref[1] = ratio
    ahead_ref[1] = part
    lead_ref[1] = first

    def forward(i, carry):
        ratio, part, first, _ = carry
        rate = rate_ref[at(i)]
        inverse = 1.0 / ((1.0 + 2.0 * rate) + rate * ratio)
        ratio = -rate * inverse
        part = (right_ref[at(i)] + rate * part) * inverse
        first = rate * first * inverse
        ratio_ref[i] = ratio
        ahead_ref[i] = part
        lead_ref[i] = first
        return ratio, part, first, inverse

    _, part, first, inverse = lax.fori_loop(
        2, rows - 1, forward, (ratio, part, first, zero), unroll=True
    )
    last = rate_ref[at(rows - 2)] * inverse
    part_ref[at(rows - 2)] = part
    first_ref[at(rows - 2)] = first
    last_ref[at(rows - 2)] = last

    def backward(j, carry):
        part, first, last = carry
        i = rows - 3 - j
        ratio = ratio_ref[i]
        part = ahead_ref[i] - ratio * part
        first = lead_ref[i] - ratio * first
        last = -ratio * last
        part_ref[at(i)] = part
        first_ref[at(i)] = first
        last_ref[at(i)] = last
        return part, first, last

    part, first, last = lax.fori_loop(0, rows - 3, backward, (part, first, last), unroll=True)
    for ref in (part_ref, first_ref, last_ref):
        ref[at(0)] = zero
        ref[at(rows - 1)] = zero
    place = place_ref[0]
    chunk_of = lax.broadcasted_iota(jnp.int32, zero.shape, 0) % chunks
    low_open = (place > 0).astype(jnp.float32)
    high_open = (place < devices - 1).astype(jnp.float32)
    low_scale = jnp.where(chunk_of == 0, low_open, 1.0)
    high_scale = jnp.where(chunk_of == chunks - 1, high_open, 1.0)
    rate_first, rate_last = rate_ref[at(0)], rate_ref[at(rows - 1)]
    part_end, first_end, last_end = (ref[at(rows - 2)] for ref in (part_ref, first_ref, last_ref))
    equations = [
        -rate_first * low_scale,
        -rate_last * first_end,
        (1.0 + 2.0 * rate_first) - rate_first * first,
        (1.0 + 2.0 * rate_last) - rate_last * last_end,
        -rate_first * last,
        -rate_last * high_scale,
        right_ref[at(0)] + rate_first * part,
        right_ref[at(rows - 1)] + rate_last * part_end,
    ]
    for index, equation in enumerate(equations):
        system_ref[pl.ds(index, sublanes, stride=len(equations))] = equation


def local_solve(place, devices, rate, right, chunks):
    planes, length, lanes = rate.shape
    rows = length // chunks
    flat = jax.ShapeDtypeStruct((planes * length, lanes), jnp.float32)
    scratch = pltpu.VMEM((rows, planes * chunks, lanes), jnp.float32)
    system = jax.ShapeDtypeStruct((planes * chunks * 8, lanes), jnp.float32)
    return pl.pallas_call(
        functools.partial(thomas_kernel, chunks, devices),
        out_shape=(flat, flat, flat, system),
        in_specs=[pl.BlockSpec(memory_space=pltpu.SMEM)]
        + [pl.BlockSpec(memory_space=pltpu.VMEM)] * 2,
        out_specs=tuple(pl.BlockSpec(memory_space=pltpu.VMEM) for _ in range(4)),
        scratch_shapes=[scratch, scratch, scratch],
    )(place.reshape(1).astype(jnp.int32), rate.reshape(planes * length, lanes), right.reshape(planes * length, lanes))


def finish_kernel(chunks, place_ref, system_ref, part_ref, first_ref, last_ref, out_ref, ratio_ref, value_ref):
    count, planes, lanes = ratio_ref.shape
    width = system_ref.shape[0] // planes
    length = part_ref.shape[0] // planes
    rows = length // chunks

    def coefficient(row, kind):
        return system_ref[pl.ds((row // 2) * 8 + kind * 2 + row % 2, planes, stride=width)]

    ratio = value = None
    for row in range(count):
        sub, diag, upper, right = (coefficient(row, kind) for kind in range(4))
        if row == 0:
            inverse = 1.0 / diag
            value = right * inverse
        else:
            inverse = 1.0 / (diag - sub * ratio)
            value = (right - sub * value) * inverse
        ratio = upper * inverse
        ratio_ref[row] = ratio
        value_ref[row] = value
    for row in range(count - 2, -1, -1):
        value = value_ref[row] - ratio_ref[row] * value
        value_ref[row] = value
    own = place_ref[0] * (2 * chunks)
    for chunk in range(chunks):
        for plane in range(planes):
            start_value = value_ref[own + 2 * chunk, pl.ds(plane, 1), :]
            end_value = value_ref[own + 2 * chunk + 1, pl.ds(plane, 1), :]
            offset = plane * length + chunk * rows
            block = pl.ds(offset, rows)
            out_ref[block] = part_ref[block] + first_ref[block] * start_value + last_ref[block] * end_value
            out_ref[pl.ds(offset, 1)] = start_value
            out_ref[pl.ds(offset + rows - 1, 1)] = end_value


def finish(place, system, part, first, last, chunks):
    planes, width, lanes = system.shape
    count = width // 8 * 2
    table = pltpu.VMEM((count, planes, lanes), jnp.float32)
    return pl.pallas_call(
        functools.partial(finish_kernel, chunks),
        out_shape=jax.ShapeDtypeStruct(part.shape, jnp.float32),
        in_specs=[pl.BlockSpec(memory_space=pltpu.SMEM)]
        + [pl.BlockSpec(memory_space=pltpu.VMEM)] * 4,
        out_specs=pl.BlockSpec(memory_space=pltpu.VMEM),
        scratch_shapes=[table, table],
    )(place.reshape(1).astype(jnp.int32), system.reshape(planes * width, lanes), part, first, last)


def shards(field, courant, diffusion_number):
    chunks = 2
    y_padded = padded_2(field, (("gy", 0),), 2, True)
    x_padded = padded_2(field, (("gx", 1),), 2, False)
    rhs = build_rhs(field, courant, y_padded, x_padded)
    place = lax.axis_index("gx")
    device_count = lax.axis_size("gx")
    planes = field.shape[0]
    part, first, last, system = local_solve(place, device_count, diffusion_number, rhs, chunks)
    lanes = field.shape[-1]
    stacked = system.reshape(planes, chunks * 8, lanes)
    gathered = lax.all_gather(stacked, "gx", axis=1, tiled=True)
    length = field.shape[1]
    solved = finish(place, gathered, part, first, last, chunks)
    return solved.reshape(planes, length, lanes)


def solution(mesh):
    in_specs = (P("gy", "gx", None), P(None, "gy", "gx", None), P("gy", "gx", None))
    out_specs = P("gy", "gx", None)
    return jax.shard_map(shards, mesh=mesh, in_specs=in_specs, out_specs=out_specs, check_vma=False)
```

```python
import functools

import jax
import jax.numpy as jnp
from jax import lax
from jax.sharding import PartitionSpec as P
from jax.experimental import pallas as pl
from jax.experimental.pallas import tpu as pltpu


def padded_2(cells, sides, width, closed):
    for axis, dim in sides:
        count = lax.axis_size(axis)
        ends = count if closed else count - 1
        head = lax.slice_in_dim(cells, 0, width, axis=dim)
        tail = lax.slice_in_dim(cells, cells.shape[dim] - width, cells.shape[dim], axis=dim)
        cells = jnp.concatenate(
            [
                lax.ppermute(tail, axis, [(i, (i + 1) % count) for i in range(ends)]),
                cells,
                lax.ppermute(head, axis, [((i + 1) % count, i) for i in range(ends)]),
            ],
            axis=dim,
        )
    return cells


def difference_pair(padded, sweep_direction, length):
    shifted = [
        lax.slice_in_dim(padded, offset, offset + length, axis=sweep_direction)
        for offset in range(5)
    ]
    gradient = (8.0 * (shifted[3] - shifted[1]) - (shifted[4] - shifted[0])) / 12.0
    curvature = (
        16.0 * (shifted[3] + shifted[1]) - (shifted[4] + shifted[0]) - 30.0 * shifted[2]
    ) / 12.0
    return (gradient, curvature)


def build_rhs(field, courant, y_padded, x_padded):
    z_padded = jnp.concatenate([field[:, :, -2:], field, field[:, :, :2]], 2)
    grad_y, curve_y = difference_pair(y_padded, 0, field.shape[0])
    grad_x = difference_pair(x_padded, 1, field.shape[1])[0]
    grad_z, curve_z = difference_pair(z_padded, 2, field.shape[2])
    transport = courant[0] * grad_x + courant[1] * grad_y + courant[2] * grad_z
    return field - transport + 0.05 * (curve_y + curve_z) + 0.3 * field / (1.0 + field * field)


def rows_below(values, stride, fill, sweep_direction):
    length = values.shape[sweep_direction]
    filler = jnp.full_like(lax.slice_in_dim(values, 0, stride, axis=sweep_direction), fill)
    return jnp.concatenate(
        [filler, lax.slice_in_dim(values, 0, length - stride, axis=sweep_direction)],
        sweep_direction,
    )


def rows_above(values, stride, fill, sweep_direction):
    length = values.shape[sweep_direction]
    filler = jnp.full_like(
        lax.slice_in_dim(values, length - stride, length, axis=sweep_direction), fill
    )
    return jnp.concatenate(
        [lax.slice_in_dim(values, stride, length, axis=sweep_direction), filler], sweep_direction
    )


def combine_rows(own_rows, below_set, above_set):
    lower_band, main_diagonal, upper_band, right_hand_sides = own_rows
    low_sub, low_diag, low_super, low_rights = below_set
    high_sub, high_diag, high_super, high_rights = above_set
    factor_low = -lower_band / low_diag
    factor_high = -upper_band / high_diag
    new_sub = factor_low * low_sub
    new_super = factor_high * high_super
    new_diag = main_diagonal + factor_low * low_super + factor_high * high_sub
    new_rights = tuple(
        (
            value + factor_low * lower_value + factor_high * upper_value
            for value, lower_value, upper_value in zip(right_hand_sides, low_rights, high_rights)
        )
    )
    return (new_sub, new_diag, new_super, new_rights)


def parallel_cyclic_reduction(
    lower_band, main_diagonal, upper_band, right_hand_sides, sweep_direction
):
    length = main_diagonal.shape[sweep_direction]
    stride = 1
    while stride < length:
        below_set = (
            rows_below(lower_band, stride, 0.0, sweep_direction),
            rows_below(main_diagonal, stride, 1.0, sweep_direction),
            rows_below(upper_band, stride, 0.0, sweep_direction),
            tuple((rows_below(value, stride, 0.0, sweep_direction) for value in right_hand_sides)),
        )
        above_set = (
            rows_above(lower_band, stride, 0.0, sweep_direction),
            rows_above(main_diagonal, stride, 1.0, sweep_direction),
            rows_above(upper_band, stride, 0.0, sweep_direction),
            tuple((rows_above(value, stride, 0.0, sweep_direction) for value in right_hand_sides)),
        )
        lower_band, main_diagonal, upper_band, right_hand_sides = combine_rows(
            (lower_band, main_diagonal, upper_band, right_hand_sides), below_set, above_set
        )
        stride = stride * 2
    return tuple((value / main_diagonal for value in right_hand_sides))


def thomas_kernel(
    chunks, devices, place_ref, rate_ref, right_ref,
    part_ref, first_ref, last_ref, system_ref, ratio_ref, ahead_ref, lead_ref,
):
    rows = ratio_ref.shape[0]
    sublanes = ratio_ref.shape[1]

    def at(i):
        return pl.ds(i, sublanes, stride=rows)

    zero = jnp.zeros(ratio_ref.shape[1:], jnp.float32)
    rate = rate_ref[at(1)]
    inverse = 1.0 / (1.0 + 2.0 * rate)
    ratio = -rate * inverse
    part = right_ref[at(1)] * inverse
    first = rate * inverse
    ratio_ref[1] = ratio
    ahead_ref[1] = part
    lead_ref[1] = first

    def forward(i, carry):
        ratio, part, first, _ = carry
        rate = rate_ref[at(i)]
        inverse = 1.0 / ((1.0 + 2.0 * rate) + rate * ratio)
        ratio = -rate * inverse
        part = (right_ref[at(i)] + rate * part) * inverse
        first = rate * first * inverse
        ratio_ref[i] = ratio
        ahead_ref[i] = part
        lead_ref[i] = first
        return ratio, part, first, inverse

    _, part, first, inverse = lax.fori_loop(
        2, rows - 1, forward, (ratio, part, first, zero), unroll=True
    )
    last = rate_ref[at(rows - 2)] * inverse
    part_ref[rows - 2] = part
    first_ref[rows - 2] = first
    last_ref[rows - 2] = last

    def backward(j, carry):
        part, first, last = carry
        i = rows - 3 - j
        ratio = ratio_ref[i]
        part = ahead_ref[i] - ratio * part
        first = lead_ref[i] - ratio * first
        last = -ratio * last
        part_ref[i] = part
        first_ref[i] = first
        last_ref[i] = last
        return part, first, last

    part, first, last = lax.fori_loop(0, rows - 3, backward, (part, first, last), unroll=True)
    for ref in (part_ref, first_ref, last_ref):
        ref[0] = zero
        ref[rows - 1] = zero
    place = place_ref[0]
    chunk_of = lax.broadcasted_iota(jnp.int32, zero.shape, 0) % chunks
    low_open = (place > 0).astype(jnp.float32)
    high_open = (place < devices - 1).astype(jnp.float32)
    low_scale = jnp.where(chunk_of == 0, low_open, 1.0)
    high_scale = jnp.where(chunk_of == chunks - 1, high_open, 1.0)
    rate_first, rate_last = rate_ref[at(0)], rate_ref[at(rows - 1)]
    part_end, first_end, last_end = (ref[rows - 2] for ref in (part_ref, first_ref, last_ref))
    equations = [
        -rate_first * low_scale,
        -rate_last * first_end,
        (1.0 + 2.0 * rate_first) - rate_first * first,
        (1.0 + 2.0 * rate_last) - rate_last * last_end,
        -rate_first * last,
        -rate_last * high_scale,
        right_ref[at(0)] + rate_first * part,
        right_ref[at(rows - 1)] + rate_last * part_end,
    ]
    for index, equation in enumerate(equations):
        system_ref[pl.ds(index, sublanes, stride=len(equations))] = equation


def local_solve(place, devices, rate, right, chunks):
    planes, length, lanes = rate.shape
    rows = length // chunks
    table = jax.ShapeDtypeStruct((rows, planes * chunks, lanes), jnp.float32)
    scratch = pltpu.VMEM((rows, planes * chunks, lanes), jnp.float32)
    system = jax.ShapeDtypeStruct((planes * chunks * 8, lanes), jnp.float32)
    return pl.pallas_call(
        functools.partial(thomas_kernel, chunks, devices),
        out_shape=(table, table, table, system),
        in_specs=[pl.BlockSpec(memory_space=pltpu.SMEM)]
        + [pl.BlockSpec(memory_space=pltpu.VMEM)] * 2,
        out_specs=tuple(pl.BlockSpec(memory_space=pltpu.VMEM) for _ in range(4)),
        scratch_shapes=[scratch, scratch, scratch],
    )(place.reshape(1).astype(jnp.int32), rate.reshape(planes * length, lanes), right.reshape(planes * length, lanes))


def finish_kernel(chunks, place_ref, system_ref, part_ref, first_ref, last_ref, out_ref, ratio_ref, value_ref):
    count, planes, lanes = ratio_ref.shape
    width = system_ref.shape[0] // planes
    rows = part_ref.shape[0] // (planes * chunks)
    length = rows * chunks

    def coefficient(row, kind):
        return system_ref[pl.ds((row // 2) * 8 + kind * 2 + row % 2, planes, stride=width)]

    ratio = value = None
    for row in range(count):
        sub, diag, upper, right = (coefficient(row, kind) for kind in range(4))
        if row == 0:
            inverse = 1.0 / diag
            value = right * inverse
        else:
            inverse = 1.0 / (diag - sub * ratio)
            value = (right - sub * value) * inverse
        ratio = upper * inverse
        ratio_ref[row] = ratio
        value_ref[row] = value
    for row in range(count - 2, -1, -1):
        value = value_ref[row] - ratio_ref[row] * value
        value_ref[row] = value
    own = place_ref[0] * (2 * chunks)
    for chunk in range(chunks):
        for plane in range(planes):
            start_value = value_ref[own + 2 * chunk, pl.ds(plane, 1), :]
            end_value = value_ref[own + 2 * chunk + 1, pl.ds(plane, 1), :]
            offset = plane * length + chunk * rows
            block = pl.ds(offset, rows)
            table = pl.ds(plane * chunks + chunk, rows, stride=planes * chunks)
            out_ref[block] = (
                part_ref[table] + first_ref[table] * start_value + last_ref[table] * end_value
            )
            out_ref[pl.ds(offset, 1)] = start_value
            out_ref[pl.ds(offset + rows - 1, 1)] = end_value


def finish(place, system, part, first, last, chunks):
    planes, width, lanes = system.shape
    count = width // 8 * 2
    table = pltpu.VMEM((count, planes, lanes), jnp.float32)
    return pl.pallas_call(
        functools.partial(finish_kernel, chunks),
        out_shape=jax.ShapeDtypeStruct((part.shape[0] * part.shape[1], lanes), jnp.float32),
        in_specs=[pl.BlockSpec(memory_space=pltpu.SMEM)]
        + [pl.BlockSpec(memory_space=pltpu.VMEM)] * 4,
        out_specs=pl.BlockSpec(memory_space=pltpu.VMEM),
        scratch_shapes=[table, table],
    )(
        place.reshape(1).astype(jnp.int32),
        system.reshape(planes * width, lanes),
        *(value.reshape(-1, lanes) for value in (part, first, last)),
    )


def shards(field, courant, diffusion_number):
    chunks = 2
    y_padded = padded_2(field, (("gy", 0),), 2, True)
    x_padded = padded_2(field, (("gx", 1),), 2, False)
    rhs = build_rhs(field, courant, y_padded, x_padded)
    place = lax.axis_index("gx")
    device_count = lax.axis_size("gx")
    planes = field.shape[0]
    part, first, last, system = local_solve(place, device_count, diffusion_number, rhs, chunks)
    lanes = field.shape[-1]
    stacked = system.reshape(planes, chunks * 8, lanes)
    gathered = lax.all_gather(stacked, "gx", axis=1, tiled=True)
    length = field.shape[1]
    solved = finish(place, gathered, part, first, last, chunks)
    return solved.reshape(planes, length, lanes)


def solution(mesh):
    in_specs = (P("gy", "gx", None), P(None, "gy", "gx", None), P("gy", "gx", None))
    out_specs = P("gy", "gx", None)
    return jax.shard_map(shards, mesh=mesh, in_specs=in_specs, out_specs=out_specs, check_vma=False)
```

```python
import functools

import jax
import jax.numpy as jnp
from jax import lax
from jax.sharding import PartitionSpec as P
from jax.experimental import pallas as pl
from jax.experimental.pallas import tpu as pltpu


def padded_2(cells, sides, width, closed):
    for axis, dim in sides:
        count = lax.axis_size(axis)
        ends = count if closed else count - 1
        head = lax.slice_in_dim(cells, 0, width, axis=dim)
        tail = lax.slice_in_dim(cells, cells.shape[dim] - width, cells.shape[dim], axis=dim)
        cells = jnp.concatenate(
            [
                lax.ppermute(tail, axis, [(i, (i + 1) % count) for i in range(ends)]),
                cells,
                lax.ppermute(head, axis, [((i + 1) % count, i) for i in range(ends)]),
            ],
            axis=dim,
        )
    return cells


def difference_pair(padded, sweep_direction, length):
    shifted = [
        lax.slice_in_dim(padded, offset, offset + length, axis=sweep_direction)
        for offset in range(5)
    ]
    gradient = (8.0 * (shifted[3] - shifted[1]) - (shifted[4] - shifted[0])) / 12.0
    curvature = (
        16.0 * (shifted[3] + shifted[1]) - (shifted[4] + shifted[0]) - 30.0 * shifted[2]
    ) / 12.0
    return (gradient, curvature)


def build_rhs(field, courant, y_padded, x_padded):
    z_padded = jnp.concatenate([field[:, :, -2:], field, field[:, :, :2]], 2)
    grad_y, curve_y = difference_pair(y_padded, 0, field.shape[0])
    grad_x = difference_pair(x_padded, 1, field.shape[1])[0]
    grad_z, curve_z = difference_pair(z_padded, 2, field.shape[2])
    transport = courant[0] * grad_x + courant[1] * grad_y + courant[2] * grad_z
    return field - transport + 0.05 * (curve_y + curve_z) + 0.3 * field / (1.0 + field * field)


def rows_below(values, stride, fill, sweep_direction):
    length = values.shape[sweep_direction]
    filler = jnp.full_like(lax.slice_in_dim(values, 0, stride, axis=sweep_direction), fill)
    return jnp.concatenate(
        [filler, lax.slice_in_dim(values, 0, length - stride, axis=sweep_direction)],
        sweep_direction,
    )


def rows_above(values, stride, fill, sweep_direction):
    length = values.shape[sweep_direction]
    filler = jnp.full_like(
        lax.slice_in_dim(values, length - stride, length, axis=sweep_direction), fill
    )
    return jnp.concatenate(
        [lax.slice_in_dim(values, stride, length, axis=sweep_direction), filler], sweep_direction
    )


def combine_rows(own_rows, below_set, above_set):
    lower_band, main_diagonal, upper_band, right_hand_sides = own_rows
    low_sub, low_diag, low_super, low_rights = below_set
    high_sub, high_diag, high_super, high_rights = above_set
    factor_low = -lower_band / low_diag
    factor_high = -upper_band / high_diag
    new_sub = factor_low * low_sub
    new_super = factor_high * high_super
    new_diag = main_diagonal + factor_low * low_super + factor_high * high_sub
    new_rights = tuple(
        (
            value + factor_low * lower_value + factor_high * upper_value
            for value, lower_value, upper_value in zip(right_hand_sides, low_rights, high_rights)
        )
    )
    return (new_sub, new_diag, new_super, new_rights)


def parallel_cyclic_reduction(
    lower_band, main_diagonal, upper_band, right_hand_sides, sweep_direction
):
    length = main_diagonal.shape[sweep_direction]
    stride = 1
    while stride < length:
        below_set = (
            rows_below(lower_band, stride, 0.0, sweep_direction),
            rows_below(main_diagonal, stride, 1.0, sweep_direction),
            rows_below(upper_band, stride, 0.0, sweep_direction),
            tuple((rows_below(value, stride, 0.0, sweep_direction) for value in right_hand_sides)),
        )
        above_set = (
            rows_above(lower_band, stride, 0.0, sweep_direction),
            rows_above(main_diagonal, stride, 1.0, sweep_direction),
            rows_above(upper_band, stride, 0.0, sweep_direction),
            tuple((rows_above(value, stride, 0.0, sweep_direction) for value in right_hand_sides)),
        )
        lower_band, main_diagonal, upper_band, right_hand_sides = combine_rows(
            (lower_band, main_diagonal, upper_band, right_hand_sides), below_set, above_set
        )
        stride = stride * 2
    return tuple((value / main_diagonal for value in right_hand_sides))


def thomas_kernel(
    chunks, devices, place_ref, rate_ref, right_ref,
    part_ref, first_ref, last_ref, system_ref, ratio_ref, ahead_ref, lead_ref,
):
    rows = ratio_ref.shape[0]
    sublanes = ratio_ref.shape[1]

    def at(i):
        return pl.ds(i, sublanes, stride=rows)

    zero = jnp.zeros(ratio_ref.shape[1:], jnp.float32)
    rate = rate_ref[at(1)]
    inverse = 1.0 / (1.0 + 2.0 * rate)
    ratio = -rate * inverse
    part = right_ref[at(1)] * inverse
    first = rate * inverse
    ratio_ref[1] = ratio
    ahead_ref[1] = part
    lead_ref[1] = first

    def forward(i, carry):
        ratio, part, first, _ = carry
        rate = rate_ref[at(i)]
        inverse = 1.0 / ((1.0 + 2.0 * rate) + rate * ratio)
        ratio = -rate * inverse
        part = (right_ref[at(i)] + rate * part) * inverse
        first = rate * first * inverse
        ratio_ref[i] = ratio
        ahead_ref[i] = part
        lead_ref[i] = first
        return ratio, part, first, inverse

    _, part, first, inverse = lax.fori_loop(
        2, rows - 1, forward, (ratio, part, first, zero), unroll=True
    )
    last = rate_ref[at(rows - 2)] * inverse
    part_ref[rows - 2] = part
    first_ref[rows - 2] = first
    last_ref[rows - 2] = last

    def backward(j, carry):
        part, first, last = carry
        i = rows - 3 - j
        ratio = ratio_ref[i]
        part = ahead_ref[i] - ratio * part
        first = lead_ref[i] - ratio * first
        last = -ratio * last
        part_ref[i] = part
        first_ref[i] = first
        last_ref[i] = last
        return part, first, last

    part, first, last = lax.fori_loop(0, rows - 3, backward, (part, first, last), unroll=True)
    for ref in (part_ref, first_ref, last_ref):
        ref[0] = zero
        ref[rows - 1] = zero
    place = place_ref[0]
    chunk_of = lax.broadcasted_iota(jnp.int32, zero.shape, 0) % chunks
    low_open = (place > 0).astype(jnp.float32)
    high_open = (place < devices - 1).astype(jnp.float32)
    low_scale = jnp.where(chunk_of == 0, low_open, 1.0)
    high_scale = jnp.where(chunk_of == chunks - 1, high_open, 1.0)
    rate_first, rate_last = rate_ref[at(0)], rate_ref[at(rows - 1)]
    part_end, first_end, last_end = (ref[rows - 2] for ref in (part_ref, first_ref, last_ref))
    equations = [
        -rate_first * low_scale,
        -rate_last * first_end,
        (1.0 + 2.0 * rate_first) - rate_first * first,
        (1.0 + 2.0 * rate_last) - rate_last * last_end,
        -rate_first * last,
        -rate_last * high_scale,
        right_ref[at(0)] + rate_first * part,
        right_ref[at(rows - 1)] + rate_last * part_end,
    ]
    for index, equation in enumerate(equations):
        system_ref[pl.ds(index, sublanes, stride=len(equations))] = equation


def local_solve(place, devices, rate, right, chunks):
    planes, length, lanes = rate.shape
    rows = length // chunks
    table = jax.ShapeDtypeStruct((rows, planes * chunks, lanes), jnp.float32)
    scratch = pltpu.VMEM((rows, planes * chunks, lanes), jnp.float32)
    system = jax.ShapeDtypeStruct((planes * chunks * 8, lanes), jnp.float32)
    return pl.pallas_call(
        functools.partial(thomas_kernel, chunks, devices),
        out_shape=(table, table, table, system),
        in_specs=[pl.BlockSpec(memory_space=pltpu.SMEM)]
        + [pl.BlockSpec(memory_space=pltpu.VMEM)] * 2,
        out_specs=tuple(pl.BlockSpec(memory_space=pltpu.VMEM) for _ in range(4)),
        scratch_shapes=[scratch, scratch, scratch],
    )(place.reshape(1).astype(jnp.int32), rate.reshape(planes * length, lanes), right.reshape(planes * length, lanes))


def finish_kernel(
    chunks, place_ref, system_ref, part_ref, first_ref, last_ref, out_ref, ratio_ref, value_ref, ends_ref
):
    count, planes, lanes = ratio_ref.shape
    width = system_ref.shape[0] // planes
    rows = part_ref.shape[0] // (planes * chunks)
    length = rows * chunks

    def coefficient(row, kind):
        return system_ref[pl.ds((row // 2) * 8 + kind * 2 + row % 2, planes, stride=width)]

    ratio = value = None
    for row in range(count):
        sub, diag, upper, right = (coefficient(row, kind) for kind in range(4))
        if row == 0:
            inverse = 1.0 / diag
            value = right * inverse
        else:
            inverse = 1.0 / (diag - sub * ratio)
            value = (right - sub * value) * inverse
        ratio = upper * inverse
        ratio_ref[row] = ratio
        value_ref[row] = value
    for row in range(count - 2, -1, -1):
        value = value_ref[row] - ratio_ref[row] * value
        value_ref[row] = value
    own = place_ref[0] * (2 * chunks)
    sublanes = planes * chunks
    for chunk in range(chunks):
        for plane in range(planes):
            lane_row = pl.ds(plane * chunks + chunk, 1)
            ends_ref[0, lane_row, :] = value_ref[own + 2 * chunk, pl.ds(plane, 1), :]
            ends_ref[1, lane_row, :] = value_ref[own + 2 * chunk + 1, pl.ds(plane, 1), :]
    start_value, end_value = ends_ref[0], ends_ref[1]

    def at(i):
        return pl.ds(i, sublanes, stride=rows)

    def combine(i, carry):
        row = pl.ds(i * sublanes, sublanes)
        out_ref[at(i)] = part_ref[row] + first_ref[row] * start_value + last_ref[row] * end_value
        return carry

    lax.fori_loop(1, rows - 1, combine, 0, unroll=8)
    out_ref[at(0)] = start_value
    out_ref[at(rows - 1)] = end_value


def finish(place, system, part, first, last, chunks):
    planes, width, lanes = system.shape
    count = width // 8 * 2
    table = pltpu.VMEM((count, planes, lanes), jnp.float32)
    return pl.pallas_call(
        functools.partial(finish_kernel, chunks),
        out_shape=jax.ShapeDtypeStruct((part.shape[0] * part.shape[1], lanes), jnp.float32),
        in_specs=[pl.BlockSpec(memory_space=pltpu.SMEM)]
        + [pl.BlockSpec(memory_space=pltpu.VMEM)] * 4,
        out_specs=pl.BlockSpec(memory_space=pltpu.VMEM),
        scratch_shapes=[table, table, pltpu.VMEM((2, planes * chunks, lanes), jnp.float32)],
    )(
        place.reshape(1).astype(jnp.int32),
        system.reshape(planes * width, lanes),
        *(value.reshape(-1, lanes) for value in (part, first, last)),
    )


def shards(field, courant, diffusion_number):
    chunks = 2
    y_padded = padded_2(field, (("gy", 0),), 2, True)
    x_padded = padded_2(field, (("gx", 1),), 2, False)
    rhs = build_rhs(field, courant, y_padded, x_padded)
    place = lax.axis_index("gx")
    device_count = lax.axis_size("gx")
    planes = field.shape[0]
    part, first, last, system = local_solve(place, device_count, diffusion_number, rhs, chunks)
    lanes = field.shape[-1]
    stacked = system.reshape(planes, chunks * 8, lanes)
    gathered = lax.all_gather(stacked, "gx", axis=1, tiled=True)
    length = field.shape[1]
    solved = finish(place, gathered, part, first, last, chunks)
    return solved.reshape(planes, length, lanes)


def solution(mesh):
    in_specs = (P("gy", "gx", None), P(None, "gy", "gx", None), P("gy", "gx", None))
    out_specs = P("gy", "gx", None)
    return jax.shard_map(shards, mesh=mesh, in_specs=in_specs, out_specs=out_specs, check_vma=False)
```

```python
import functools

import jax
import jax.numpy as jnp
from jax import lax
from jax.sharding import PartitionSpec as P
from jax.experimental import pallas as pl
from jax.experimental.pallas import tpu as pltpu


def padded_2(cells, sides, width, closed):
    for axis, dim in sides:
        count = lax.axis_size(axis)
        ends = count if closed else count - 1
        head = lax.slice_in_dim(cells, 0, width, axis=dim)
        tail = lax.slice_in_dim(cells, cells.shape[dim] - width, cells.shape[dim], axis=dim)
        cells = jnp.concatenate(
            [
                lax.ppermute(tail, axis, [(i, (i + 1) % count) for i in range(ends)]),
                cells,
                lax.ppermute(head, axis, [((i + 1) % count, i) for i in range(ends)]),
            ],
            axis=dim,
        )
    return cells


def difference_pair(padded, sweep_direction, length):
    shifted = [
        lax.slice_in_dim(padded, offset, offset + length, axis=sweep_direction)
        for offset in range(5)
    ]
    gradient = (8.0 * (shifted[3] - shifted[1]) - (shifted[4] - shifted[0])) / 12.0
    curvature = (
        16.0 * (shifted[3] + shifted[1]) - (shifted[4] + shifted[0]) - 30.0 * shifted[2]
    ) / 12.0
    return (gradient, curvature)


def build_rhs(field, courant, y_padded, x_padded):
    z_padded = jnp.concatenate([field[:, :, -2:], field, field[:, :, :2]], 2)
    grad_y, curve_y = difference_pair(y_padded, 0, field.shape[0])
    grad_x = difference_pair(x_padded, 1, field.shape[1])[0]
    grad_z, curve_z = difference_pair(z_padded, 2, field.shape[2])
    transport = courant[0] * grad_x + courant[1] * grad_y + courant[2] * grad_z
    return field - transport + 0.05 * (curve_y + curve_z) + 0.3 * field / (1.0 + field * field)


def rows_below(values, stride, fill, sweep_direction):
    length = values.shape[sweep_direction]
    filler = jnp.full_like(lax.slice_in_dim(values, 0, stride, axis=sweep_direction), fill)
    return jnp.concatenate(
        [filler, lax.slice_in_dim(values, 0, length - stride, axis=sweep_direction)],
        sweep_direction,
    )


def rows_above(values, stride, fill, sweep_direction):
    length = values.shape[sweep_direction]
    filler = jnp.full_like(
        lax.slice_in_dim(values, length - stride, length, axis=sweep_direction), fill
    )
    return jnp.concatenate(
        [lax.slice_in_dim(values, stride, length, axis=sweep_direction), filler], sweep_direction
    )


def combine_rows(own_rows, below_set, above_set):
    lower_band, main_diagonal, upper_band, right_hand_sides = own_rows
    low_sub, low_diag, low_super, low_rights = below_set
    high_sub, high_diag, high_super, high_rights = above_set
    factor_low = -lower_band / low_diag
    factor_high = -upper_band / high_diag
    new_sub = factor_low * low_sub
    new_super = factor_high * high_super
    new_diag = main_diagonal + factor_low * low_super + factor_high * high_sub
    new_rights = tuple(
        (
            value + factor_low * lower_value + factor_high * upper_value
            for value, lower_value, upper_value in zip(right_hand_sides, low_rights, high_rights)
        )
    )
    return (new_sub, new_diag, new_super, new_rights)


def parallel_cyclic_reduction(
    lower_band, main_diagonal, upper_band, right_hand_sides, sweep_direction
):
    length = main_diagonal.shape[sweep_direction]
    stride = 1
    while stride < length:
        below_set = (
            rows_below(lower_band, stride, 0.0, sweep_direction),
            rows_below(main_diagonal, stride, 1.0, sweep_direction),
            rows_below(upper_band, stride, 0.0, sweep_direction),
            tuple((rows_below(value, stride, 0.0, sweep_direction) for value in right_hand_sides)),
        )
        above_set = (
            rows_above(lower_band, stride, 0.0, sweep_direction),
            rows_above(main_diagonal, stride, 1.0, sweep_direction),
            rows_above(upper_band, stride, 0.0, sweep_direction),
            tuple((rows_above(value, stride, 0.0, sweep_direction) for value in right_hand_sides)),
        )
        lower_band, main_diagonal, upper_band, right_hand_sides = combine_rows(
            (lower_band, main_diagonal, upper_band, right_hand_sides), below_set, above_set
        )
        stride = stride * 2
    return tuple((value / main_diagonal for value in right_hand_sides))


def thomas_kernel(
    chunks, devices, place_ref, rate_ref, right_ref,
    part_ref, first_ref, last_ref, system_ref, ratio_ref, ahead_ref, lead_ref,
):
    rows = ratio_ref.shape[0]
    sublanes = ratio_ref.shape[1]

    def at(i):
        return pl.ds(i, sublanes, stride=rows)

    zero = jnp.zeros(ratio_ref.shape[1:], jnp.float32)
    rate = rate_ref[at(1)]
    inverse = 1.0 / (1.0 + 2.0 * rate)
    ratio = -rate * inverse
    part = right_ref[at(1)] * inverse
    first = rate * inverse
    ratio_ref[1] = ratio
    ahead_ref[1] = part
    lead_ref[1] = first

    def forward(i, carry):
        ratio, part, first, _ = carry
        rate = rate_ref[at(i)]
        inverse = 1.0 / ((1.0 + 2.0 * rate) + rate * ratio)
        ratio = -rate * inverse
        part = (right_ref[at(i)] + rate * part) * inverse
        first = rate * first * inverse
        ratio_ref[i] = ratio
        ahead_ref[i] = part
        lead_ref[i] = first
        return ratio, part, first, inverse

    _, part, first, inverse = lax.fori_loop(
        2, rows - 1, forward, (ratio, part, first, zero), unroll=True
    )
    last = rate_ref[at(rows - 2)] * inverse
    part_ref[rows - 2] = part
    first_ref[rows - 2] = first
    last_ref[rows - 2] = last

    def backward(j, carry):
        part, first, last = carry
        i = rows - 3 - j
        ratio = ratio_ref[i]
        part = ahead_ref[i] - ratio * part
        first = lead_ref[i] - ratio * first
        last = -ratio * last
        part_ref[i] = part
        first_ref[i] = first
        last_ref[i] = last
        return part, first, last

    part, first, last = lax.fori_loop(0, rows - 3, backward, (part, first, last), unroll=True)
    for ref in (part_ref, first_ref, last_ref):
        ref[0] = zero
        ref[rows - 1] = zero
    place = place_ref[0]
    chunk_of = lax.broadcasted_iota(jnp.int32, zero.shape, 0) % chunks
    low_open = (place > 0).astype(jnp.float32)
    high_open = (place < devices - 1).astype(jnp.float32)
    low_scale = jnp.where(chunk_of == 0, low_open, 1.0)
    high_scale = jnp.where(chunk_of == chunks - 1, high_open, 1.0)
    rate_first, rate_last = rate_ref[at(0)], rate_ref[at(rows - 1)]
    part_end, first_end, last_end = (ref[rows - 2] for ref in (part_ref, first_ref, last_ref))
    equations = [
        -rate_first * low_scale,
        -rate_last * first_end,
        (1.0 + 2.0 * rate_first) - rate_first * first,
        (1.0 + 2.0 * rate_last) - rate_last * last_end,
        -rate_first * last,
        -rate_last * high_scale,
        right_ref[at(0)] + rate_first * part,
        right_ref[at(rows - 1)] + rate_last * part_end,
    ]
    for index, equation in enumerate(equations):
        system_ref[pl.ds(index, sublanes, stride=len(equations))] = equation


def local_solve(place, devices, rate, right, chunks):
    planes, length, lanes = rate.shape
    rows = length // chunks
    table = jax.ShapeDtypeStruct((rows, planes * chunks, lanes), jnp.float32)
    scratch = pltpu.VMEM((rows, planes * chunks, lanes), jnp.float32)
    system = jax.ShapeDtypeStruct((planes * chunks * 8, lanes), jnp.float32)
    return pl.pallas_call(
        functools.partial(thomas_kernel, chunks, devices),
        out_shape=(table, table, table, system),
        in_specs=[pl.BlockSpec(memory_space=pltpu.SMEM)]
        + [pl.BlockSpec(memory_space=pltpu.VMEM)] * 2,
        out_specs=tuple(pl.BlockSpec(memory_space=pltpu.VMEM) for _ in range(4)),
        scratch_shapes=[scratch, scratch, scratch],
    )(place.reshape(1).astype(jnp.int32), rate.reshape(planes * length, lanes), right.reshape(planes * length, lanes))


def finish_kernel(
    chunks, place_ref, system_ref, part_ref, first_ref, last_ref, out_ref, ratio_ref, value_ref, ends_ref
):
    count, planes, lanes = ratio_ref.shape
    width = system_ref.shape[0] // planes
    rows = part_ref.shape[0] // (planes * chunks)
    length = rows * chunks

    def coefficient(row, kind):
        return system_ref[pl.ds((row // 2) * 8 + kind * 2 + row % 2, planes, stride=width)]

    middle = count // 2
    ratio = value = back_ratio = back_value = None
    for step in range(middle):
        row, back = step, count - 1 - step
        sub, diag, upper, right = (coefficient(row, kind) for kind in range(4))
        if step == 0:
            inverse = 1.0 / diag
            value = right * inverse
        else:
            inverse = 1.0 / (diag - sub * ratio)
            value = (right - sub * value) * inverse
        ratio = upper * inverse
        ratio_ref[row] = ratio
        value_ref[row] = value
        sub, diag, upper, right = (coefficient(back, kind) for kind in range(4))
        if step == 0:
            inverse = 1.0 / diag
            back_value = right * inverse
        else:
            inverse = 1.0 / (diag - upper * back_ratio)
            back_value = (right - upper * back_value) * inverse
        back_ratio = sub * inverse
        ratio_ref[back] = back_ratio
        value_ref[back] = back_value
    value = (value - ratio * back_value) / (1.0 - ratio * back_ratio)
    back_value = back_value - back_ratio * value
    value_ref[middle - 1] = value
    value_ref[middle] = back_value
    for step in range(1, middle):
        row, back = middle - 1 - step, middle + step
        value = value_ref[row] - ratio_ref[row] * value
        value_ref[row] = value
        back_value = value_ref[back] - ratio_ref[back] * back_value
        value_ref[back] = back_value
    own = place_ref[0] * (2 * chunks)
    sublanes = planes * chunks
    for chunk in range(chunks):
        for plane in range(planes):
            lane_row = pl.ds(plane * chunks + chunk, 1)
            ends_ref[0, lane_row, :] = value_ref[own + 2 * chunk, pl.ds(plane, 1), :]
            ends_ref[1, lane_row, :] = value_ref[own + 2 * chunk + 1, pl.ds(plane, 1), :]
    start_value, end_value = ends_ref[0], ends_ref[1]

    def at(i):
        return pl.ds(i, sublanes, stride=rows)

    def combine(i, carry):
        row = pl.ds(i * sublanes, sublanes)
        out_ref[at(i)] = part_ref[row] + first_ref[row] * start_value + last_ref[row] * end_value
        return carry

    lax.fori_loop(1, rows - 1, combine, 0, unroll=8)
    out_ref[at(0)] = start_value
    out_ref[at(rows - 1)] = end_value


def finish(place, system, part, first, last, chunks):
    planes, width, lanes = system.shape
    count = width // 8 * 2
    table = pltpu.VMEM((count, planes, lanes), jnp.float32)
    return pl.pallas_call(
        functools.partial(finish_kernel, chunks),
        out_shape=jax.ShapeDtypeStruct((part.shape[0] * part.shape[1], lanes), jnp.float32),
        in_specs=[pl.BlockSpec(memory_space=pltpu.SMEM)]
        + [pl.BlockSpec(memory_space=pltpu.VMEM)] * 4,
        out_specs=pl.BlockSpec(memory_space=pltpu.VMEM),
        scratch_shapes=[table, table, pltpu.VMEM((2, planes * chunks, lanes), jnp.float32)],
    )(
        place.reshape(1).astype(jnp.int32),
        system.reshape(planes * width, lanes),
        *(value.reshape(-1, lanes) for value in (part, first, last)),
    )


def shards(field, courant, diffusion_number):
    chunks = 2
    y_padded = padded_2(field, (("gy", 0),), 2, True)
    x_padded = padded_2(field, (("gx", 1),), 2, False)
    rhs = build_rhs(field, courant, y_padded, x_padded)
    place = lax.axis_index("gx")
    device_count = lax.axis_size("gx")
    planes = field.shape[0]
    part, first, last, system = local_solve(place, device_count, diffusion_number, rhs, chunks)
    lanes = field.shape[-1]
    stacked = system.reshape(planes, chunks * 8, lanes)
    gathered = lax.all_gather(stacked, "gx", axis=1, tiled=True)
    length = field.shape[1]
    solved = finish(place, gathered, part, first, last, chunks)
    return solved.reshape(planes, length, lanes)


def solution(mesh):
    in_specs = (P("gy", "gx", None), P(None, "gy", "gx", None), P("gy", "gx", None))
    out_specs = P("gy", "gx", None)
    return jax.shard_map(shards, mesh=mesh, in_specs=in_specs, out_specs=out_specs, check_vma=False)
```

```python
import functools

import jax
import jax.numpy as jnp
from jax import lax
from jax.sharding import PartitionSpec as P
from jax.experimental import pallas as pl
from jax.experimental.pallas import tpu as pltpu


def padded_2(cells, sides, width, closed):
    for axis, dim in sides:
        count = lax.axis_size(axis)
        ends = count if closed else count - 1
        head = lax.slice_in_dim(cells, 0, width, axis=dim)
        tail = lax.slice_in_dim(cells, cells.shape[dim] - width, cells.shape[dim], axis=dim)
        cells = jnp.concatenate(
            [
                lax.ppermute(tail, axis, [(i, (i + 1) % count) for i in range(ends)]),
                cells,
                lax.ppermute(head, axis, [((i + 1) % count, i) for i in range(ends)]),
            ],
            axis=dim,
        )
    return cells


def difference_pair(padded, sweep_direction, length):
    shifted = [
        lax.slice_in_dim(padded, offset, offset + length, axis=sweep_direction)
        for offset in range(5)
    ]
    gradient = (8.0 * (shifted[3] - shifted[1]) - (shifted[4] - shifted[0])) / 12.0
    curvature = (
        16.0 * (shifted[3] + shifted[1]) - (shifted[4] + shifted[0]) - 30.0 * shifted[2]
    ) / 12.0
    return (gradient, curvature)


def build_rhs(field, courant, y_padded, x_padded):
    z_padded = jnp.concatenate([field[:, :, -2:], field, field[:, :, :2]], 2)
    grad_y, curve_y = difference_pair(y_padded, 0, field.shape[0])
    grad_x = difference_pair(x_padded, 1, field.shape[1])[0]
    grad_z, curve_z = difference_pair(z_padded, 2, field.shape[2])
    transport = courant[0] * grad_x + courant[1] * grad_y + courant[2] * grad_z
    return field - transport + 0.05 * (curve_y + curve_z) + 0.3 * field / (1.0 + field * field)


def rows_below(values, stride, fill, sweep_direction):
    length = values.shape[sweep_direction]
    filler = jnp.full_like(lax.slice_in_dim(values, 0, stride, axis=sweep_direction), fill)
    return jnp.concatenate(
        [filler, lax.slice_in_dim(values, 0, length - stride, axis=sweep_direction)],
        sweep_direction,
    )


def rows_above(values, stride, fill, sweep_direction):
    length = values.shape[sweep_direction]
    filler = jnp.full_like(
        lax.slice_in_dim(values, length - stride, length, axis=sweep_direction), fill
    )
    return jnp.concatenate(
        [lax.slice_in_dim(values, stride, length, axis=sweep_direction), filler], sweep_direction
    )


def combine_rows(own_rows, below_set, above_set):
    lower_band, main_diagonal, upper_band, right_hand_sides = own_rows
    low_sub, low_diag, low_super, low_rights = below_set
    high_sub, high_diag, high_super, high_rights = above_set
    factor_low = -lower_band / low_diag
    factor_high = -upper_band / high_diag
    new_sub = factor_low * low_sub
    new_super = factor_high * high_super
    new_diag = main_diagonal + factor_low * low_super + factor_high * high_sub
    new_rights = tuple(
        (
            value + factor_low * lower_value + factor_high * upper_value
            for value, lower_value, upper_value in zip(right_hand_sides, low_rights, high_rights)
        )
    )
    return (new_sub, new_diag, new_super, new_rights)


def parallel_cyclic_reduction(
    lower_band, main_diagonal, upper_band, right_hand_sides, sweep_direction
):
    length = main_diagonal.shape[sweep_direction]
    stride = 1
    while stride < length:
        below_set = (
            rows_below(lower_band, stride, 0.0, sweep_direction),
            rows_below(main_diagonal, stride, 1.0, sweep_direction),
            rows_below(upper_band, stride, 0.0, sweep_direction),
            tuple((rows_below(value, stride, 0.0, sweep_direction) for value in right_hand_sides)),
        )
        above_set = (
            rows_above(lower_band, stride, 0.0, sweep_direction),
            rows_above(main_diagonal, stride, 1.0, sweep_direction),
            rows_above(upper_band, stride, 0.0, sweep_direction),
            tuple((rows_above(value, stride, 0.0, sweep_direction) for value in right_hand_sides)),
        )
        lower_band, main_diagonal, upper_band, right_hand_sides = combine_rows(
            (lower_band, main_diagonal, upper_band, right_hand_sides), below_set, above_set
        )
        stride = stride * 2
    return tuple((value / main_diagonal for value in right_hand_sides))


def thomas_kernel(
    chunks, devices, place_ref, rate_ref, right_ref,
    part_ref, first_ref, last_ref, system_ref, ratio_ref, ahead_ref, lead_ref,
):
    rows = ratio_ref.shape[0]
    sublanes = ratio_ref.shape[1]

    def at(i):
        return pl.ds(i, sublanes, stride=rows)

    zero = jnp.zeros(ratio_ref.shape[1:], jnp.float32)
    top, bottom = 1, rows - 2
    middle = (top + bottom + 1) // 2
    rate = rate_ref[at(top)]
    inverse = 1.0 / (1.0 + 2.0 * rate)
    ratio = -rate * inverse
    part = right_ref[at(top)] * inverse
    first = rate * inverse
    ratio_ref[top] = ratio
    ahead_ref[top] = part
    lead_ref[top] = first
    rate = rate_ref[at(bottom)]
    inverse = 1.0 / (1.0 + 2.0 * rate)
    back_ratio = -rate * inverse
    back_part = right_ref[at(bottom)] * inverse
    last = rate * inverse
    ratio_ref[bottom] = back_ratio
    ahead_ref[bottom] = back_part
    lead_ref[bottom] = last

    def forward(step, carry):
        ratio, part, first, back_ratio, back_part, last = carry
        i = top + step
        rate = rate_ref[at(i)]
        inverse = 1.0 / ((1.0 + 2.0 * rate) + rate * ratio)
        ratio = -rate * inverse
        part = (right_ref[at(i)] + rate * part) * inverse
        first = rate * first * inverse
        ratio_ref[i] = ratio
        ahead_ref[i] = part
        lead_ref[i] = first
        k = bottom - step
        rate = rate_ref[at(k)]
        inverse = 1.0 / ((1.0 + 2.0 * rate) + rate * back_ratio)
        back_ratio = -rate * inverse
        back_part = (right_ref[at(k)] + rate * back_part) * inverse
        last = rate * last * inverse
        ratio_ref[k] = back_ratio
        ahead_ref[k] = back_part
        lead_ref[k] = last
        return ratio, part, first, back_ratio, back_part, last

    ratio, part, first, back_ratio, back_part, last = lax.fori_loop(
        1, middle - top, forward, (ratio, part, first, back_ratio, back_part, last), unroll=True
    )
    scale = 1.0 / (1.0 - ratio * back_ratio)
    part = (part - ratio * back_part) * scale
    first = first * scale
    last_top = -ratio * last * scale
    back_part = back_part - back_ratio * part
    back_first = -back_ratio * first
    last = last - back_ratio * last_top
    part_ref[middle - 1], first_ref[middle - 1], last_ref[middle - 1] = part, first, last_top
    part_ref[middle], first_ref[middle], last_ref[middle] = back_part, back_first, last

    def backward(step, carry):
        part, first, last_top, back_part, back_first, last = carry
        i = middle - 1 - step
        ratio = ratio_ref[i]
        part = ahead_ref[i] - ratio * part
        first = lead_ref[i] - ratio * first
        last_top = -ratio * last_top
        part_ref[i], first_ref[i], last_ref[i] = part, first, last_top
        k = middle + step
        back_ratio = ratio_ref[k]
        back_part = ahead_ref[k] - back_ratio * back_part
        back_first = -back_ratio * back_first
        last = lead_ref[k] - back_ratio * last
        part_ref[k], first_ref[k], last_ref[k] = back_part, back_first, last
        return part, first, last_top, back_part, back_first, last

    part, first, last, _, _, _ = lax.fori_loop(
        1, middle - top, backward, (part, first, last_top, back_part, back_first, last), unroll=True
    )
    for ref in (part_ref, first_ref, last_ref):
        ref[0] = zero
        ref[rows - 1] = zero
    place = place_ref[0]
    chunk_of = lax.broadcasted_iota(jnp.int32, zero.shape, 0) % chunks
    low_open = (place > 0).astype(jnp.float32)
    high_open = (place < devices - 1).astype(jnp.float32)
    low_scale = jnp.where(chunk_of == 0, low_open, 1.0)
    high_scale = jnp.where(chunk_of == chunks - 1, high_open, 1.0)
    rate_first, rate_last = rate_ref[at(0)], rate_ref[at(rows - 1)]
    part_end, first_end, last_end = (ref[rows - 2] for ref in (part_ref, first_ref, last_ref))
    equations = [
        -rate_first * low_scale,
        -rate_last * first_end,
        (1.0 + 2.0 * rate_first) - rate_first * first,
        (1.0 + 2.0 * rate_last) - rate_last * last_end,
        -rate_first * last,
        -rate_last * high_scale,
        right_ref[at(0)] + rate_first * part,
        right_ref[at(rows - 1)] + rate_last * part_end,
    ]
    for index, equation in enumerate(equations):
        system_ref[pl.ds(index, sublanes, stride=len(equations))] = equation


def local_solve(place, devices, rate, right, chunks):
    planes, length, lanes = rate.shape
    rows = length // chunks
    table = jax.ShapeDtypeStruct((rows, planes * chunks, lanes), jnp.float32)
    scratch = pltpu.VMEM((rows, planes * chunks, lanes), jnp.float32)
    system = jax.ShapeDtypeStruct((planes * chunks * 8, lanes), jnp.float32)
    return pl.pallas_call(
        functools.partial(thomas_kernel, chunks, devices),
        out_shape=(table, table, table, system),
        in_specs=[pl.BlockSpec(memory_space=pltpu.SMEM)]
        + [pl.BlockSpec(memory_space=pltpu.VMEM)] * 2,
        out_specs=tuple(pl.BlockSpec(memory_space=pltpu.VMEM) for _ in range(4)),
        scratch_shapes=[scratch, scratch, scratch],
    )(place.reshape(1).astype(jnp.int32), rate.reshape(planes * length, lanes), right.reshape(planes * length, lanes))


def finish_kernel(
    chunks, place_ref, system_ref, part_ref, first_ref, last_ref, out_ref, ratio_ref, value_ref, ends_ref
):
    count, planes, lanes = ratio_ref.shape
    width = system_ref.shape[0] // planes
    rows = part_ref.shape[0] // (planes * chunks)
    length = rows * chunks

    def coefficient(row, kind):
        return system_ref[pl.ds((row // 2) * 8 + kind * 2 + row % 2, planes, stride=width)]

    middle = count // 2
    ratio = value = back_ratio = back_value = None
    for step in range(middle):
        row, back = step, count - 1 - step
        sub, diag, upper, right = (coefficient(row, kind) for kind in range(4))
        if step == 0:
            inverse = 1.0 / diag
            value = right * inverse
        else:
            inverse = 1.0 / (diag - sub * ratio)
            value = (right - sub * value) * inverse
        ratio = upper * inverse
        ratio_ref[row] = ratio
        value_ref[row] = value
        sub, diag, upper, right = (coefficient(back, kind) for kind in range(4))
        if step == 0:
            inverse = 1.0 / diag
            back_value = right * inverse
        else:
            inverse = 1.0 / (diag - upper * back_ratio)
            back_value = (right - upper * back_value) * inverse
        back_ratio = sub * inverse
        ratio_ref[back] = back_ratio
        value_ref[back] = back_value
    value = (value - ratio * back_value) / (1.0 - ratio * back_ratio)
    back_value = back_value - back_ratio * value
    value_ref[middle - 1] = value
    value_ref[middle] = back_value
    for step in range(1, middle):
        row, back = middle - 1 - step, middle + step
        value = value_ref[row] - ratio_ref[row] * value
        value_ref[row] = value
        back_value = value_ref[back] - ratio_ref[back] * back_value
        value_ref[back] = back_value
    own = place_ref[0] * (2 * chunks)
    sublanes = planes * chunks
    for chunk in range(chunks):
        for plane in range(planes):
            lane_row = pl.ds(plane * chunks + chunk, 1)
            ends_ref[0, lane_row, :] = value_ref[own + 2 * chunk, pl.ds(plane, 1), :]
            ends_ref[1, lane_row, :] = value_ref[own + 2 * chunk + 1, pl.ds(plane, 1), :]
    start_value, end_value = ends_ref[0], ends_ref[1]

    def at(i):
        return pl.ds(i, sublanes, stride=rows)

    def combine(i, carry):
        row = pl.ds(i * sublanes, sublanes)
        out_ref[at(i)] = part_ref[row] + first_ref[row] * start_value + last_ref[row] * end_value
        return carry

    lax.fori_loop(1, rows - 1, combine, 0, unroll=8)
    out_ref[at(0)] = start_value
    out_ref[at(rows - 1)] = end_value


def finish(place, system, part, first, last, chunks):
    planes, width, lanes = system.shape
    count = width // 8 * 2
    table = pltpu.VMEM((count, planes, lanes), jnp.float32)
    return pl.pallas_call(
        functools.partial(finish_kernel, chunks),
        out_shape=jax.ShapeDtypeStruct((part.shape[0] * part.shape[1], lanes), jnp.float32),
        in_specs=[pl.BlockSpec(memory_space=pltpu.SMEM)]
        + [pl.BlockSpec(memory_space=pltpu.VMEM)] * 4,
        out_specs=pl.BlockSpec(memory_space=pltpu.VMEM),
        scratch_shapes=[table, table, pltpu.VMEM((2, planes * chunks, lanes), jnp.float32)],
    )(
        place.reshape(1).astype(jnp.int32),
        system.reshape(planes * width, lanes),
        *(value.reshape(-1, lanes) for value in (part, first, last)),
    )


def shards(field, courant, diffusion_number):
    chunks = 2
    y_padded = padded_2(field, (("gy", 0),), 2, True)
    x_padded = padded_2(field, (("gx", 1),), 2, False)
    rhs = build_rhs(field, courant, y_padded, x_padded)
    place = lax.axis_index("gx")
    device_count = lax.axis_size("gx")
    planes = field.shape[0]
    part, first, last, system = local_solve(place, device_count, diffusion_number, rhs, chunks)
    lanes = field.shape[-1]
    stacked = system.reshape(planes, chunks * 8, lanes)
    gathered = lax.all_gather(stacked, "gx", axis=1, tiled=True)
    length = field.shape[1]
    solved = finish(place, gathered, part, first, last, chunks)
    return solved.reshape(planes, length, lanes)


def solution(mesh):
    in_specs = (P("gy", "gx", None), P(None, "gy", "gx", None), P("gy", "gx", None))
    out_specs = P("gy", "gx", None)
    return jax.shard_map(shards, mesh=mesh, in_specs=in_specs, out_specs=out_specs, check_vma=False)
```

```python
import functools

import jax
import jax.numpy as jnp
from jax import lax
from jax.sharding import PartitionSpec as P
from jax.experimental import pallas as pl
from jax.experimental.pallas import tpu as pltpu


def padded_2(cells, sides, width, closed):
    for axis, dim in sides:
        count = lax.axis_size(axis)
        ends = count if closed else count - 1
        head = lax.slice_in_dim(lax.optimization_barrier(cells), 0, width, axis=dim)
        tail = lax.slice_in_dim(cells, cells.shape[dim] - width, cells.shape[dim], axis=dim)
        cells = jnp.concatenate(
            [
                lax.ppermute(tail, axis, [(i, (i + 1) % count) for i in range(ends)]),
                cells,
                lax.ppermute(head, axis, [((i + 1) % count, i) for i in range(ends)]),
            ],
            axis=dim,
        )
    return cells


def difference_pair(padded, sweep_direction, length):
    shifted = [
        lax.slice_in_dim(padded, offset, offset + length, axis=sweep_direction)
        for offset in range(5)
    ]
    gradient = (8.0 * (shifted[3] - shifted[1]) - (shifted[4] - shifted[0])) / 12.0
    curvature = (
        16.0 * (shifted[3] + shifted[1]) - (shifted[4] + shifted[0]) - 30.0 * shifted[2]
    ) / 12.0
    return (gradient, curvature)


def build_rhs(field, courant, y_padded, x_padded):
    z_padded = jnp.concatenate([field[:, :, -2:], field, field[:, :, :2]], 2)
    grad_y, curve_y = difference_pair(y_padded, 0, field.shape[0])
    grad_x = difference_pair(x_padded, 1, field.shape[1])[0]
    grad_z, curve_z = difference_pair(z_padded, 2, field.shape[2])
    transport = courant[0] * grad_x + courant[1] * grad_y + courant[2] * grad_z
    return field - transport + 0.05 * (curve_y + curve_z) + 0.3 * field / (1.0 + field * field)


def rows_below(values, stride, fill, sweep_direction):
    length = values.shape[sweep_direction]
    filler = jnp.full_like(lax.slice_in_dim(values, 0, stride, axis=sweep_direction), fill)
    return jnp.concatenate(
        [filler, lax.slice_in_dim(values, 0, length - stride, axis=sweep_direction)],
        sweep_direction,
    )


def rows_above(values, stride, fill, sweep_direction):
    length = values.shape[sweep_direction]
    filler = jnp.full_like(
        lax.slice_in_dim(values, length - stride, length, axis=sweep_direction), fill
    )
    return jnp.concatenate(
        [lax.slice_in_dim(values, stride, length, axis=sweep_direction), filler], sweep_direction
    )


def combine_rows(own_rows, below_set, above_set):
    lower_band, main_diagonal, upper_band, right_hand_sides = own_rows
    low_sub, low_diag, low_super, low_rights = below_set
    high_sub, high_diag, high_super, high_rights = above_set
    factor_low = -lower_band / low_diag
    factor_high = -upper_band / high_diag
    new_sub = factor_low * low_sub
    new_super = factor_high * high_super
    new_diag = main_diagonal + factor_low * low_super + factor_high * high_sub
    new_rights = tuple(
        (
            value + factor_low * lower_value + factor_high * upper_value
            for value, lower_value, upper_value in zip(right_hand_sides, low_rights, high_rights)
        )
    )
    return (new_sub, new_diag, new_super, new_rights)


def parallel_cyclic_reduction(
    lower_band, main_diagonal, upper_band, right_hand_sides, sweep_direction
):
    length = main_diagonal.shape[sweep_direction]
    stride = 1
    while stride < length:
        below_set = (
            rows_below(lower_band, stride, 0.0, sweep_direction),
            rows_below(main_diagonal, stride, 1.0, sweep_direction),
            rows_below(upper_band, stride, 0.0, sweep_direction),
            tuple((rows_below(value, stride, 0.0, sweep_direction) for value in right_hand_sides)),
        )
        above_set = (
            rows_above(lower_band, stride, 0.0, sweep_direction),
            rows_above(main_diagonal, stride, 1.0, sweep_direction),
            rows_above(upper_band, stride, 0.0, sweep_direction),
            tuple((rows_above(value, stride, 0.0, sweep_direction) for value in right_hand_sides)),
        )
        lower_band, main_diagonal, upper_band, right_hand_sides = combine_rows(
            (lower_band, main_diagonal, upper_band, right_hand_sides), below_set, above_set
        )
        stride = stride * 2
    return tuple((value / main_diagonal for value in right_hand_sides))


def thomas_kernel(
    chunks, devices, place_ref, rate_ref, right_ref,
    part_ref, first_ref, last_ref, system_ref, ratio_ref, ahead_ref, lead_ref,
):
    rows = ratio_ref.shape[0]
    sublanes = ratio_ref.shape[1]

    def at(i):
        return pl.ds(i, sublanes, stride=rows)

    zero = jnp.zeros(ratio_ref.shape[1:], jnp.float32)
    top, bottom = 1, rows - 2
    middle = (top + bottom + 1) // 2
    rate = rate_ref[at(top)]
    inverse = 1.0 / (1.0 + 2.0 * rate)
    ratio = -rate * inverse
    part = right_ref[at(top)] * inverse
    first = rate * inverse
    ratio_ref[top] = ratio
    ahead_ref[top] = part
    lead_ref[top] = first
    rate = rate_ref[at(bottom)]
    inverse = 1.0 / (1.0 + 2.0 * rate)
    back_ratio = -rate * inverse
    back_part = right_ref[at(bottom)] * inverse
    last = rate * inverse
    ratio_ref[bottom] = back_ratio
    ahead_ref[bottom] = back_part
    lead_ref[bottom] = last

    def forward(step, carry):
        ratio, part, first, back_ratio, back_part, last = carry
        i = top + step
        rate = rate_ref[at(i)]
        inverse = 1.0 / ((1.0 + 2.0 * rate) + rate * ratio)
        ratio = -rate * inverse
        part = (right_ref[at(i)] + rate * part) * inverse
        first = rate * first * inverse
        ratio_ref[i] = ratio
        ahead_ref[i] = part
        lead_ref[i] = first
        k = bottom - step
        rate = rate_ref[at(k)]
        inverse = 1.0 / ((1.0 + 2.0 * rate) + rate * back_ratio)
        back_ratio = -rate * inverse
        back_part = (right_ref[at(k)] + rate * back_part) * inverse
        last = rate * last * inverse
        ratio_ref[k] = back_ratio
        ahead_ref[k] = back_part
        lead_ref[k] = last
        return ratio, part, first, back_ratio, back_part, last

    ratio, part, first, back_ratio, back_part, last = lax.fori_loop(
        1, middle - top, forward, (ratio, part, first, back_ratio, back_part, last), unroll=True
    )
    scale = 1.0 / (1.0 - ratio * back_ratio)
    part = (part - ratio * back_part) * scale
    first = first * scale
    last_top = -ratio * last * scale
    back_part = back_part - back_ratio * part
    back_first = -back_ratio * first
    last = last - back_ratio * last_top
    part_ref[middle - 1], first_ref[middle - 1], last_ref[middle - 1] = part, first, last_top
    part_ref[middle], first_ref[middle], last_ref[middle] = back_part, back_first, last

    def backward(step, carry):
        part, first, last_top, back_part, back_first, last = carry
        i = middle - 1 - step
        ratio = ratio_ref[i]
        part = ahead_ref[i] - ratio * part
        first = lead_ref[i] - ratio * first
        last_top = -ratio * last_top
        part_ref[i], first_ref[i], last_ref[i] = part, first, last_top
        k = middle + step
        back_ratio = ratio_ref[k]
        back_part = ahead_ref[k] - back_ratio * back_part
        back_first = -back_ratio * back_first
        last = lead_ref[k] - back_ratio * last
        part_ref[k], first_ref[k], last_ref[k] = back_part, back_first, last
        return part, first, last_top, back_part, back_first, last

    part, first, last, _, _, _ = lax.fori_loop(
        1, middle - top, backward, (part, first, last_top, back_part, back_first, last), unroll=True
    )
    for ref in (part_ref, first_ref, last_ref):
        ref[0] = zero
        ref[rows - 1] = zero
    place = place_ref[0]
    chunk_of = lax.broadcasted_iota(jnp.int32, zero.shape, 0) % chunks
    low_open = (place > 0).astype(jnp.float32)
    high_open = (place < devices - 1).astype(jnp.float32)
    low_scale = jnp.where(chunk_of == 0, low_open, 1.0)
    high_scale = jnp.where(chunk_of == chunks - 1, high_open, 1.0)
    rate_first, rate_last = rate_ref[at(0)], rate_ref[at(rows - 1)]
    part_end, first_end, last_end = (ref[rows - 2] for ref in (part_ref, first_ref, last_ref))
    equations = [
        -rate_first * low_scale,
        -rate_last * first_end,
        (1.0 + 2.0 * rate_first) - rate_first * first,
        (1.0 + 2.0 * rate_last) - rate_last * last_end,
        -rate_first * last,
        -rate_last * high_scale,
        right_ref[at(0)] + rate_first * part,
        right_ref[at(rows - 1)] + rate_last * part_end,
    ]
    for index, equation in enumerate(equations):
        system_ref[pl.ds(index, sublanes, stride=len(equations))] = equation


def local_solve(place, devices, rate, right, chunks):
    planes, length, lanes = rate.shape
    rows = length // chunks
    table = jax.ShapeDtypeStruct((rows, planes * chunks, lanes), jnp.float32)
    scratch = pltpu.VMEM((rows, planes * chunks, lanes), jnp.float32)
    system = jax.ShapeDtypeStruct((planes * chunks * 8, lanes), jnp.float32)
    return pl.pallas_call(
        functools.partial(thomas_kernel, chunks, devices),
        out_shape=(table, table, table, system),
        in_specs=[pl.BlockSpec(memory_space=pltpu.SMEM)]
        + [pl.BlockSpec(memory_space=pltpu.VMEM)] * 2,
        out_specs=tuple(pl.BlockSpec(memory_space=pltpu.VMEM) for _ in range(4)),
        scratch_shapes=[scratch, scratch, scratch],
    )(place.reshape(1).astype(jnp.int32), rate.reshape(planes * length, lanes), right.reshape(planes * length, lanes))


def finish_kernel(
    chunks, place_ref, system_ref, part_ref, first_ref, last_ref, out_ref, ratio_ref, value_ref, ends_ref
):
    count, planes, lanes = ratio_ref.shape
    width = system_ref.shape[0] // planes
    rows = part_ref.shape[0] // (planes * chunks)
    length = rows * chunks

    def coefficient(row, kind):
        return system_ref[pl.ds((row // 2) * 8 + kind * 2 + row % 2, planes, stride=width)]

    middle = count // 2
    ratio = value = back_ratio = back_value = None
    for step in range(middle):
        row, back = step, count - 1 - step
        sub, diag, upper, right = (coefficient(row, kind) for kind in range(4))
        if step == 0:
            inverse = 1.0 / diag
            value = right * inverse
        else:
            inverse = 1.0 / (diag - sub * ratio)
            value = (right - sub * value) * inverse
        ratio = upper * inverse
        ratio_ref[row] = ratio
        value_ref[row] = value
        sub, diag, upper, right = (coefficient(back, kind) for kind in range(4))
        if step == 0:
            inverse = 1.0 / diag
            back_value = right * inverse
        else:
            inverse = 1.0 / (diag - upper * back_ratio)
            back_value = (right - upper * back_value) * inverse
        back_ratio = sub * inverse
        ratio_ref[back] = back_ratio
        value_ref[back] = back_value
    value = (value - ratio * back_value) / (1.0 - ratio * back_ratio)
    back_value = back_value - back_ratio * value
    value_ref[middle - 1] = value
    value_ref[middle] = back_value
    for step in range(1, middle):
        row, back = middle - 1 - step, middle + step
        value = value_ref[row] - ratio_ref[row] * value
        value_ref[row] = value
        back_value = value_ref[back] - ratio_ref[back] * back_value
        value_ref[back] = back_value
    own = place_ref[0] * (2 * chunks)
    sublanes = planes * chunks
    for chunk in range(chunks):
        for plane in range(planes):
            lane_row = pl.ds(plane * chunks + chunk, 1)
            ends_ref[0, lane_row, :] = value_ref[own + 2 * chunk, pl.ds(plane, 1), :]
            ends_ref[1, lane_row, :] = value_ref[own + 2 * chunk + 1, pl.ds(plane, 1), :]
    start_value, end_value = ends_ref[0], ends_ref[1]

    def at(i):
        return pl.ds(i, sublanes, stride=rows)

    def combine(i, carry):
        row = pl.ds(i * sublanes, sublanes)
        out_ref[at(i)] = part_ref[row] + first_ref[row] * start_value + last_ref[row] * end_value
        return carry

    lax.fori_loop(1, rows - 1, combine, 0, unroll=8)
    out_ref[at(0)] = start_value
    out_ref[at(rows - 1)] = end_value


def finish(place, system, part, first, last, chunks):
    planes, width, lanes = system.shape
    count = width // 8 * 2
    table = pltpu.VMEM((count, planes, lanes), jnp.float32)
    return pl.pallas_call(
        functools.partial(finish_kernel, chunks),
        out_shape=jax.ShapeDtypeStruct((part.shape[0] * part.shape[1], lanes), jnp.float32),
        in_specs=[pl.BlockSpec(memory_space=pltpu.SMEM)]
        + [pl.BlockSpec(memory_space=pltpu.VMEM)] * 4,
        out_specs=pl.BlockSpec(memory_space=pltpu.VMEM),
        scratch_shapes=[table, table, pltpu.VMEM((2, planes * chunks, lanes), jnp.float32)],
    )(
        place.reshape(1).astype(jnp.int32),
        system.reshape(planes * width, lanes),
        *(value.reshape(-1, lanes) for value in (part, first, last)),
    )


def shards(field, courant, diffusion_number):
    chunks = 2
    y_padded = padded_2(field, (("gy", 0),), 2, True)
    x_padded = padded_2(field, (("gx", 1),), 2, False)
    rhs = build_rhs(field, courant, y_padded, x_padded)
    place = lax.axis_index("gx")
    device_count = lax.axis_size("gx")
    planes = field.shape[0]
    part, first, last, system = local_solve(place, device_count, diffusion_number, rhs, chunks)
    lanes = field.shape[-1]
    stacked = system.reshape(planes, chunks * 8, lanes)
    gathered = lax.all_gather(stacked, "gx", axis=1, tiled=True)
    length = field.shape[1]
    solved = finish(place, gathered, part, first, last, chunks)
    return solved.reshape(planes, length, lanes)


def solution(mesh):
    in_specs = (P("gy", "gx", None), P(None, "gy", "gx", None), P("gy", "gx", None))
    out_specs = P("gy", "gx", None)
    return jax.shard_map(shards, mesh=mesh, in_specs=in_specs, out_specs=out_specs, check_vma=False)
```
